32 devices in a mesh: dp: 8 (over z, core), ctx: 4 (over y, x).
Axes of the slice: x: 2, y: 2, z: 4, core: 2. Of those that a mesh axis runs over, the one named last changes fastest.
Arguments:
- hidden: bfloat16 [8, 512, 3072], P('dp', 'ctx'), may hold values from -6 to 6
- gating: bfloat16 [8, 512, 3072], P('dp', 'ctx'), may hold values from -6 to 6
- dt_raw: bfloat16 [8, 512, 48], P('dp', 'ctx'), may hold values from -4 to 4
- b_input: bfloat16 [8, 512, 128], P('dp', 'ctx'), may hold values from -0.5 to 0.5
- c_input: bfloat16 [8, 512, 128], P('dp', 'ctx'), may hold values from -0.5 to 0.5
- resets: int32 [8, 2], P('dp'), may hold values 0 or 1
- cotangent: bfloat16 [8, 512, 3072], P('dp', 'ctx'), may hold values from -18 to 18
- parameters: float32 [3216], replicated, may hold values from -10 to 2
- adam_mean: float32 [8, 804], P('dp'), may hold values from -6 to 6
- adam_square: float32 [8, 804], P('dp'), may hold values from 0.1 to 2
- bucket_size: int32 [8], replicated, may hold values from 1 to 804, 3216 in all
- bucket_owner: int32 [8], replicated, may hold values from 0 to 7, each once
Outputs:
- normed: bfloat16 [8, 512, 3072], P('dp', 'ctx')
- grad_hidden: bfloat16 [8, 512, 3072], P('dp', 'ctx')
- grad_gating: bfloat16 [8, 512, 3072], P('dp', 'ctx')
- grad_dt: bfloat16 [8, 512, 48], P('dp', 'ctx')
- grad_b: bfloat16 [8, 512, 128], P('dp', 'ctx')
- grad_c: bfloat16 [8, 512, 128], P('dp', 'ctx')
- new_params: float32 [3216], replicated
- new_mean: float32 [8, 804], P('dp')
- new_square: float32 [8, 804], P('dp')
The draws below stay inside these ranges and needn't reach their ends.
Inputs may be any that keep to these rules, and one draw needn't show every extreme that they name: `bucket_size`: the sizes sum to 3216; the largest is exactly 804. `bucket_owner`: each dp index owns exactly one bucket.
All inputs are finite; a program needn't handle non-finite values. No bound on the sum of `resets` on one device may be relied on, other than what follows from the above.
Results may differ from the reference program's by a relative error of at most 0.0076.
Values may be sent and summed in bfloat16 or wider, within the bound.
No kernel may reach another device: no remote copies, remote signals or barrier semaphores. Data moves between devices by JAX's collectives and lax.ppermute only.
A program may use at most 128 MiB of HBM per device.

```python
import math
import jax
import jax.numpy as jnp
import numpy as np
from jax import lax

H = 48
P_SIZE = 64
N = 128
SPAN = 256
SEQ = 512
SEQS = 8
CH = 3072
F = 3216
CAP = 804
NCH = 2
N_CTX = 4


def draw_cotangent(key, part):
    place = jnp.arange(SEQS * SEQ, dtype=jnp.float32).reshape(SEQS, SEQ, 1) / (SEQS * SEQ)
    base = jnp.clip(jax.random.normal(key, (SEQS, SEQ, CH), jnp.float32), -6.0, 6.0)
    factor = 1.0 + 2.0 * place
    return (base * factor).astype(jnp.bfloat16)


def draw_parameters(key, part):
    keys = jax.random.split(key, 4)
    low = jnp.log(0.5 / SEQ)
    high = jnp.log(1.0 / 32.0)
    gain = jax.random.uniform(keys[3], (CH,), jnp.float32, 0.5, 1.5)
    a_log = jax.random.uniform(keys[0], (H,), jnp.float32, 0.0, 1.0) * (high - low) + low
    dt_bias = jax.random.uniform(keys[1], (H,), jnp.float32, -1.0, 1.0)
    skip = jax.random.uniform(keys[2], (H,), jnp.float32, 0.5, 1.5)
    return jnp.concatenate([a_log, dt_bias, skip, gain])


def set_ends(array, own_key, low, largest):
    dims = array.shape
    index_at = [jax.random.randint(jax.random.fold_in(own_key, axis), (), 0, dims[axis]) for axis in range(len(dims))]
    array = array.at[tuple(index_at)].set(low)
    longest = dims.index(max(dims))
    index_at[longest] = (index_at[longest] + 1) % dims[longest]
    return array.at[tuple(index_at)].set(largest)


def steps_of(stream_key, shape, pieces, least, top_value):
    factor_of, own = 1.0, jax.random.fold_in(stream_key, 6)
    for dim, shards_of in pieces:
        draws = jnp.exp(jax.random.uniform(jax.random.fold_in(own, dim), (shards_of,), jnp.float32, least / len(pieces), top_value / len(pieces)))
        factor_of = factor_of * jnp.repeat(draws, shape[dim] // shards_of).reshape([-1 if axis == dim else 1 for axis in range(len(shape))])
    return factor_of


def split_up(amount, total, reach, skew):
    portions = [(1 << 20) // math.isqrt(standing ** skew) + 1 for standing in range(2, amount + 1)]
    surplus, counts = total - reach - (amount - 1), [1] * (amount - 1)
    while surplus > 0:
        candidates = [i for i in range(amount - 1) if counts[i] < reach]
        mass, remaining = sum([portions[i] for i in candidates]), surplus
        for i in candidates:
            addition = min(reach - counts[i], max(1, remaining * portions[i] // mass), surplus)
            counts[i] = counts[i] + addition
            surplus = surplus - addition
    return np.array([reach] + counts)


def uneven(own_key, number_of, total, bound, skew):
    if number_of == 2:
        one = jax.random.randint(own_key, (), max(1, total - bound), min(bound, total - 1) + 1)
        return jnp.stack([one, total - one])
    tallies = jnp.asarray(split_up(number_of, total, bound, skew), jnp.int32)
    twos = (number_of - 1) // 2
    giver, sink = tallies[1:1 + 2 * twos:2], tallies[2:2 + 2 * twos:2]
    margin = jnp.minimum(giver - 1, bound - sink)
    passed = jax.random.randint(jax.random.fold_in(own_key, 1), (twos,), 0, 1 << 20) % (margin + 1)
    tallies = tallies.at[1:1 + 2 * twos:2].set(giver - passed).at[2:2 + 2 * twos:2].set(sink + passed)
    return tallies[jax.random.permutation(jax.random.fold_in(own_key, 2), number_of)]


def noise(own_key, dims, scale, limit, pieces=(), held_as=jnp.bfloat16):
    values = jax.random.normal(own_key, dims, jnp.float32) * scale
    if len(pieces) > 0:
        values = steps_of(own_key, dims, pieces, -0.22, 0.18) * values
    return jnp.clip(values, min=-limit, max=limit).astype(held_as)


def setup_inputs(seed: int = 0) -> dict:
    arg_keys = jax.random.split(jax.random.key(seed), 13)
    hidden = noise(arg_keys[0], (SEQS, SEQ, CH), 1.0, 6.0, ((0, 8), (1, 4)))
    gating = noise(arg_keys[1], (SEQS, SEQ, CH), 1.0, 6.0, ((0, 8), (1, 4)))
    dt_raw = noise(arg_keys[2], (SEQS, SEQ, H), 1.0, 4.0, ((0, 8), (1, 4)))
    b_input = noise(arg_keys[3], (SEQS, SEQ, N), N ** -0.5, 0.5, ((0, 8), (1, 4)))
    c_input = noise(arg_keys[4], (SEQS, SEQ, N), N ** -0.5, 0.5, ((0, 8), (1, 4)))
    resets = set_ends((jax.random.randint(arg_keys[5], (SEQS, NCH), 0, 3) < 1).astype(jnp.int32), jax.random.fold_in(arg_keys[5], 1), 0, 1)
    cotangent = draw_cotangent(jax.random.fold_in(arg_keys[12], 71), 0)
    parameters = draw_parameters(jax.random.fold_in(arg_keys[12], 71), 0)
    adam_mean = noise(arg_keys[8], (SEQS, CAP), 1.0, 6.0, ((0, 8),), jnp.float32)
    adam_square = jnp.clip(jnp.exp(math.log(2.0) - 2.9957323 * jax.random.uniform(arg_keys[9], (SEQS, CAP), jnp.float32) ** steps_of(arg_keys[9], (SEQS, CAP), ((0, 8),), -0.2, 0.2)), 0.1, 2.0)
    bucket_size = uneven(arg_keys[10], SEQS, F, CAP, 2).astype(jnp.int32)
    bucket_owner = jax.random.permutation(arg_keys[11], SEQS).astype(jnp.int32)
    return {"hidden": hidden, "gating": gating, "dt_raw": dt_raw, "b_input": b_input, "c_input": c_input, "resets": resets, "cotangent": cotangent, "parameters": parameters, "adam_mean": adam_mean, "adam_square": adam_square, "bucket_size": bucket_size, "bucket_owner": bucket_owner}


eps_norm = 1e-05
clip_norm = 64.0
beta_one = 0.9
beta_two = 0.95
adam_eps = 1e-08
learn_rate = 0.02
step_count = 100.0
highest = lax.Precision.HIGHEST

def rounded(value):
    return lax.optimization_barrier(value.astype(jnp.bfloat16)).astype(jnp.float32)

def ssd_group(hidden, dt_raw, b_input, c_input, resets, a_log, dt_bias, skip):
    length = hidden.shape[0]
    heads = a_log.shape[0]
    width = hidden.shape[1] // heads
    blocks = length // SPAN
    step_sizes = jax.nn.softplus(dt_raw.astype(jnp.float32) + dt_bias)
    log_decay = (step_sizes * -jnp.exp(a_log)).reshape(blocks, SPAN, heads).transpose(0, 2, 1)
    cumul = jnp.cumsum(log_decay, axis=2)
    inputs = hidden.astype(jnp.float32).reshape(blocks, SPAN, heads, width)
    scaled = rounded(inputs * step_sizes.reshape(blocks, SPAN, heads, 1))
    b_rows = b_input.astype(jnp.float32).reshape(blocks, SPAN, -1)
    c_rows = c_input.astype(jnp.float32).reshape(blocks, SPAN, -1)
    scores = jnp.einsum('ctn,csn->cts', c_rows, b_rows, precision=highest)
    causal = jnp.arange(SPAN)[:, None] >= jnp.arange(SPAN)[None, :]
    spread = cumul[:, :, :, None] - cumul[:, :, None, :]
    decay = jnp.where(causal, jnp.exp(jnp.where(causal, spread, 0.0)), 0.0)
    weights = rounded(scores[:, None] * decay)
    intra = jnp.einsum('chts,cshp->cthp', weights, scaled, precision=highest)
    tail = cumul[:, :, -1:] - cumul
    b_decayed = rounded(b_rows[:, None] * jnp.exp(tail)[..., None])
    block_state = jnp.einsum('chsn,cshp->chnp', b_decayed, scaled, precision=highest)
    keep = 1.0 - resets.astype(jnp.float32)

    def advance(state, items):
        keep_one, total, added = items
        entering = state * keep_one
        return (jnp.exp(total)[:, None, None] * entering + added, entering)
    start_state = jnp.zeros(block_state.shape[1:], jnp.float32)
    last_state, entering = lax.scan(advance, start_state, (keep, cumul[:, :, -1], block_state))
    c_decayed = rounded(c_rows[:, None] * jnp.exp(cumul)[..., None])
    inter = jnp.einsum('chtn,chnp->cthp', c_decayed, rounded(entering), precision=highest)
    output = intra + inter + skip[:, None] * inputs
    return output.reshape(length, heads * width).astype(jnp.bfloat16)

def gate_values(y_values, gating):
    gated = y_values.astype(jnp.float32) * jax.nn.silu(gating.astype(jnp.float32))
    return (gated, lax.optimization_barrier(jnp.sum(gated * gated, axis=-1)))

def normalize(gated, total, gain):
    factor = lax.rsqrt(total / CH + eps_norm)
    return (factor, (gated * factor[..., None] * gain).astype(jnp.bfloat16))

def norm_backward(cotangent, gain, gated, factor, dot_total, y_values, gating):
    upstream = cotangent.astype(jnp.float32) * gain
    d_gated = upstream * factor[..., None] - gated * (factor * factor * factor * dot_total / CH)[..., None]
    gate_f = gating.astype(jnp.float32)
    sigma = jax.nn.sigmoid(gate_f)
    d_y = (d_gated * (gate_f * sigma)).astype(jnp.bfloat16)
    d_gate = (d_gated * y_values.astype(jnp.float32) * sigma * (1.0 + gate_f * (1.0 - sigma))).astype(jnp.bfloat16)
    d_gain = lax.optimization_barrier(jnp.sum(cotangent.astype(jnp.float32) * gated * factor[..., None], axis=tuple(range(gated.ndim - 1))))
    return (d_y, d_gate, d_gain)

def reference(hidden, gating, dt_raw, b_input, c_input, resets, cotangent, parameters, adam_mean, adam_square, bucket_size, bucket_owner):
    group = H // N_CTX
    head_params = parameters[:3 * H].reshape(3, H)
    gain = parameters[3 * H:]

    def one_sequence(items):
        hid_one, gate_one, dt_one, b_one, c_one, reset_one, cot_one = items

        def slices(index):
            x_part = lax.dynamic_slice_in_dim(hid_one, index * group * P_SIZE, group * P_SIZE, 1)
            dt_part = lax.dynamic_slice_in_dim(dt_one, index * group, group, 1)
            par_part = lax.dynamic_slice_in_dim(head_params, index * group, group, 1)
            return (x_part, dt_part, par_part)

        def forward_group(index):
            x_part, dt_part, par_part = slices(index)
            return ssd_group(x_part, dt_part, b_one, c_one, reset_one, par_part[0], par_part[1], par_part[2])
        outs_groups = lax.map(forward_group, jnp.arange(N_CTX, dtype=jnp.int32))
        y_full = outs_groups.transpose(1, 0, 2).reshape(SEQ, CH)
        gated, total = gate_values(y_full, gate_one)
        factor, normed = normalize(gated, total, gain)
        dot_total = lax.optimization_barrier(jnp.sum(cot_one.astype(jnp.float32) * gain * gated, axis=-1))
        d_y, d_gate, d_gain = norm_backward(cot_one, gain, gated, factor, dot_total, y_full, gate_one)

        def backward_group(index):
            x_part, dt_part, par_part = slices(index)
            upstream = lax.dynamic_slice_in_dim(d_y, index * group * P_SIZE, group * P_SIZE, 1)

            def local_fn(x_arg, dt_arg, b_arg, c_arg, a_arg, bias_arg, skip_arg):
                return ssd_group(x_arg, dt_arg, b_arg, c_arg, reset_one, a_arg, bias_arg, skip_arg)
            primal, pullback = jax.vjp(local_fn, x_part, dt_part, b_one, c_one, par_part[0], par_part[1], par_part[2])
            return pullback(upstream)
        d_x, d_dt, d_b, d_c, d_alog, d_bias, d_skip = lax.map(backward_group, jnp.arange(N_CTX, dtype=jnp.int32))
        grad_x = d_x.transpose(1, 0, 2).reshape(SEQ, CH)
        grad_dt_one = d_dt.transpose(1, 0, 2).reshape(SEQ, H)
        grad_b_one = lax.optimization_barrier(jnp.sum(d_b.astype(jnp.float32), axis=0)).astype(jnp.bfloat16)
        grad_c_one = lax.optimization_barrier(jnp.sum(d_c.astype(jnp.float32), axis=0)).astype(jnp.bfloat16)
        grad_vec = jnp.concatenate([d_alog.reshape(H), d_bias.reshape(H), d_skip.reshape(H), d_gain])
        return (normed, grad_x, d_gate, grad_dt_one, grad_b_one, grad_c_one, grad_vec)
    normed, grad_hidden, grad_gating, grad_dt, grad_b, grad_c, grad_vecs = lax.map(one_sequence, (hidden, gating, dt_raw, b_input, c_input, resets, cotangent))
    gradient = lax.optimization_barrier(jnp.sum(grad_vecs, axis=0))
    grad_norm = jnp.sqrt(jnp.sum(gradient * gradient))
    shrink = jnp.minimum(1.0, clip_norm / (grad_norm + 1e-06))
    ends = jnp.cumsum(bucket_size)
    begins = ends - bucket_size
    order = jnp.arange(SEQS, dtype=jnp.int32)
    owned_bucket = lax.optimization_barrier(jnp.sum(jnp.where(bucket_owner[None, :] == order[:, None], order[None, :], 0), axis=1))
    row_begin = lax.optimization_barrier(jnp.sum(jnp.where(order[None, :] == owned_bucket[:, None], begins[None, :], 0), axis=1))
    row_size = lax.optimization_barrier(jnp.sum(jnp.where(order[None, :] == owned_bucket[:, None], bucket_size[None, :], 0), axis=1))
    slots = jnp.arange(CAP, dtype=jnp.int32)
    positions = row_begin[:, None] + slots[None, :]
    valid = slots[None, :] < row_size[:, None]
    padding = jnp.zeros((CAP,), jnp.float32)
    grad_rows = jnp.where(valid, jnp.concatenate([gradient, padding])[positions], 0.0) * shrink
    param_rows = jnp.where(valid, jnp.concatenate([parameters, padding])[positions], 0.0)
    new_mean = beta_one * adam_mean + (1.0 - beta_one) * grad_rows
    new_square = beta_two * adam_square + (1.0 - beta_two) * grad_rows * grad_rows
    direction = new_mean / (1.0 - beta_one ** step_count) / (jnp.sqrt(new_square / (1.0 - beta_two ** step_count)) + adam_eps)
    new_rows = param_rows - learn_rate * direction
    flat = jnp.arange(F, dtype=jnp.int32)
    bucket_of = lax.optimization_barrier(jnp.sum((ends[None, :] <= flat[:, None]).astype(jnp.int32), axis=1))
    match = order[None, :] == bucket_of[:, None]
    owner_of = lax.optimization_barrier(jnp.sum(jnp.where(match, bucket_owner[None, :], 0), axis=1))
    offset = flat - lax.optimization_barrier(jnp.sum(jnp.where(match, begins[None, :], 0), axis=1))
    new_params = new_rows.reshape(-1)[owner_of * CAP + offset]
    return (normed, grad_hidden, grad_gating, grad_dt, grad_b, grad_c, new_params, new_mean, new_square)
```

```python
import jax
import jax.numpy as jnp
from jax import lax
from jax.sharding import PartitionSpec as P

SPAN = 256
CH = 3072


eps_norm = 1e-05
clip_norm = 64.0
beta_one = 0.9
beta_two = 0.95
adam_eps = 1e-08
learn_rate = 0.02
step_count = 100.0
highest = lax.Precision.HIGHEST


def rounded(value):
    return lax.optimization_barrier(value.astype(jnp.bfloat16)).astype(jnp.float32)


def ssd_group(hidden, dt_raw, b_input, c_input, resets, a_log, dt_bias, skip):
    length = hidden.shape[0]
    heads = a_log.shape[0]
    width = hidden.shape[1] // heads
    blocks = length // SPAN
    step_sizes = jax.nn.softplus(dt_raw.astype(jnp.float32) + dt_bias)
    log_decay = (step_sizes * -jnp.exp(a_log)).reshape(blocks, SPAN, heads).transpose(0, 2, 1)
    cumul = jnp.cumsum(log_decay, axis=2)
    inputs = hidden.astype(jnp.float32).reshape(blocks, SPAN, heads, width)
    scaled = rounded(inputs * step_sizes.reshape(blocks, SPAN, heads, 1))
    b_rows = b_input.astype(jnp.float32).reshape(blocks, SPAN, -1)
    c_rows = c_input.astype(jnp.float32).reshape(blocks, SPAN, -1)
    scores = jnp.einsum("ctn,csn->cts", c_rows, b_rows, precision=highest)
    causal = jnp.arange(SPAN)[:, None] >= jnp.arange(SPAN)[None, :]
    spread = cumul[:, :, :, None] - cumul[:, :, None, :]
    decay = jnp.where(causal, jnp.exp(jnp.where(causal, spread, 0.0)), 0.0)
    weights = rounded(scores[:, None] * decay)
    intra = jnp.einsum("chts,cshp->cthp", weights, scaled, precision=highest)
    tail = cumul[:, :, -1:] - cumul
    b_decayed = rounded(b_rows[:, None] * jnp.exp(tail)[..., None])
    block_state = jnp.einsum("chsn,cshp->chnp", b_decayed, scaled, precision=highest)
    keep = 1.0 - resets.astype(jnp.float32)

    def advance(state, items):
        keep_one, total, added = items
        entering = state * keep_one
        return (jnp.exp(total)[:, None, None] * entering + added, entering)

    start_state = jnp.zeros(block_state.shape[1:], jnp.float32)
    last_state, entering = lax.scan(advance, start_state, (keep, cumul[:, :, -1], block_state))
    c_decayed = rounded(c_rows[:, None] * jnp.exp(cumul)[..., None])
    inter = jnp.einsum("chtn,chnp->cthp", c_decayed, rounded(entering), precision=highest)
    output = intra + inter + skip[:, None] * inputs
    return output.reshape(length, heads * width).astype(jnp.bfloat16)


def gate_values(y_values, gating):
    gated = y_values.astype(jnp.float32) * jax.nn.silu(gating.astype(jnp.float32))
    return (gated, jnp.sum(gated * gated, axis=-1))


def normalize(gated, total, gain):
    factor = lax.rsqrt(total / CH + eps_norm)
    return (factor, (gated * factor[..., None] * gain).astype(jnp.bfloat16))


def norm_backward(cotangent, gain, gated, factor, dot_total, y_values, gating):
    upstream = cotangent.astype(jnp.float32) * gain
    d_gated = (
        upstream * factor[..., None]
        - gated * (factor * factor * factor * dot_total / CH)[..., None]
    )
    gate_f = gating.astype(jnp.float32)
    sigma = jax.nn.sigmoid(gate_f)
    d_y = (d_gated * (gate_f * sigma)).astype(jnp.bfloat16)
    d_gate = (
        d_gated * y_values.astype(jnp.float32) * sigma * (1.0 + gate_f * (1.0 - sigma))
    ).astype(jnp.bfloat16)
    d_gain = jnp.sum(
        cotangent.astype(jnp.float32) * gated * factor[..., None], axis=tuple(range(gated.ndim - 1))
    )
    return (d_y, d_gate, d_gain)


def on_device(
    hidden,
    gating,
    dt_raw,
    b_input,
    c_input,
    resets,
    cotangent,
    parameters,
    adam_mean,
    adam_square,
    bucket_size,
    bucket_owner,
):
    heads_all = dt_raw.shape[2]
    groups = lax.axis_size("ctx")
    group = heads_all // groups
    state_size = b_input.shape[2]
    tokens = hidden.shape[1]
    first = lax.axis_index("ctx") * group
    head_params = parameters[: 3 * heads_all].reshape(3, heads_all)
    gain = parameters[3 * heads_all :]
    local_params = lax.dynamic_slice_in_dim(head_params, first, group, 1)
    b_all, c_all = (
        lax.all_gather(b_input, "ctx", axis=1, tiled=True),
        lax.all_gather(c_input, "ctx", axis=1, tiled=True),
    )
    seq_resets = resets[0]
    owners_n = lax.axis_size("dp")
    cap_n = adam_mean.shape[1]
    len_n = parameters.shape[0]
    state_all = lax.all_gather(jnp.stack([adam_mean[0], adam_square[0]]), "dp", axis=0)
    starts = jnp.cumsum(bucket_size) - bucket_size
    laid = jnp.zeros((2, len_n + cap_n), jnp.float32)
    for k in range(owners_n):
        laid = lax.dynamic_update_slice(laid, state_all[bucket_owner[k]], (0, starts[k]))
    mean_flat = laid[0, :len_n]
    square_flat = laid[1, :len_n]

    def local_fn(x_arg, dt_arg, b_arg, c_arg, a_arg, bias_arg, skip_arg):
        return ssd_group(x_arg, dt_arg, b_arg, c_arg, seq_resets, a_arg, bias_arg, skip_arg)

    x_heads, dt_heads = (
        lax.all_to_all(hidden, "ctx", split_axis=2, concat_axis=1, tiled=True),
        lax.all_to_all(dt_raw, "ctx", split_axis=2, concat_axis=1, tiled=True),
    )
    y_heads, pullback = jax.vjp(
        local_fn,
        x_heads[0],
        dt_heads[0],
        b_all[0],
        c_all[0],
        local_params[0],
        local_params[1],
        local_params[2],
    )
    y_seq = lax.all_to_all(y_heads[None], "ctx", split_axis=1, concat_axis=2, tiled=True)
    gated, total = gate_values(y_seq, gating)
    factor, normed = normalize(gated, total, gain)
    dot_total = jnp.sum(cotangent.astype(jnp.float32) * gain * gated, axis=-1)
    d_y, grad_gating, d_gain = norm_backward(
        cotangent, gain, gated, factor, dot_total, y_seq, gating
    )
    d_y_heads = lax.all_to_all(d_y, "ctx", split_axis=2, concat_axis=1, tiled=True)
    d_x, d_dt, d_b, d_c, d_alog, d_bias, d_skip = pullback(d_y_heads[0])
    d_pair = jnp.concatenate([d_b, d_c], axis=-1)
    grad_hidden, grad_dt, pair_parts = (
        lax.all_to_all(d_x[None], "ctx", split_axis=1, concat_axis=2, tiled=True),
        lax.all_to_all(d_dt[None], "ctx", split_axis=1, concat_axis=2, tiled=True),
        lax.all_to_all(d_pair[None], "ctx", split_axis=1, concat_axis=2, tiled=True),
    )
    pair_sum = jnp.sum(
        pair_parts.reshape(1, tokens, groups, 2 * state_size).astype(jnp.float32), axis=2
    ).astype(jnp.bfloat16)
    grad_b = pair_sum[..., :state_size]
    grad_c = pair_sum[..., state_size:]
    head_grads = jnp.stack([d_alog, d_bias, d_skip])
    full_heads = lax.dynamic_update_slice(
        jnp.zeros((3, heads_all), jnp.float32), head_grads, (0, first)
    )
    grad_part = jnp.concatenate([full_heads.reshape(-1), d_gain])
    gradient = lax.psum(grad_part, ("dp", "ctx"))
    grad_norm = jnp.sqrt(jnp.sum(gradient * gradient))
    shrink = jnp.minimum(1.0, clip_norm / (grad_norm + 1e-06))
    owners = lax.axis_size("dp")
    slot_cap = adam_mean.shape[1]
    total_len = parameters.shape[0]
    ends = jnp.cumsum(bucket_size)
    begins = ends - bucket_size
    order = jnp.arange(owners, dtype=jnp.int32)
    mine = lax.axis_index("dp")
    my_bucket = jnp.sum(jnp.where(bucket_owner == mine, order, 0))
    row_begin = jnp.sum(jnp.where(order == my_bucket, begins, 0))
    row_size = jnp.sum(jnp.where(order == my_bucket, bucket_size, 0))
    slots = jnp.arange(slot_cap, dtype=jnp.int32)
    valid = slots < row_size
    padding = jnp.zeros((slot_cap,), jnp.float32)
    grad_row = (
        jnp.where(
            valid,
            lax.dynamic_slice_in_dim(jnp.concatenate([gradient, padding]), row_begin, slot_cap),
            0.0,
        )
        * shrink
    )
    new_mean = beta_one * adam_mean[0] + (1.0 - beta_one) * grad_row
    new_square = beta_two * adam_square[0] + (1.0 - beta_two) * grad_row * grad_row
    grad_flat = gradient * shrink
    mean_all = beta_one * mean_flat + (1.0 - beta_one) * grad_flat
    square_all = beta_two * square_flat + (1.0 - beta_two) * grad_flat * grad_flat
    direction = (
        mean_all
        / (1.0 - beta_one**step_count)
        / (jnp.sqrt(square_all / (1.0 - beta_two**step_count)) + adam_eps)
    )
    new_params = parameters - learn_rate * direction
    return (
        normed,
        grad_hidden,
        grad_gating,
        grad_dt,
        grad_b,
        grad_c,
        new_params,
        new_mean[None],
        new_square[None],
    )


def solution(mesh):
    return jax.shard_map(
        on_device,
        mesh=mesh,
        in_specs=(
            P("dp", "ctx", None),
            P("dp", "ctx", None),
            P("dp", "ctx", None),
            P("dp", "ctx", None),
            P("dp", "ctx", None),
            P("dp", None),
            P("dp", "ctx", None),
            P(),
            P("dp", None),
            P("dp", None),
            P(),
            P(),
        ),
        out_specs=(
            P("dp", "ctx", None),
            P("dp", "ctx", None),
            P("dp", "ctx", None),
            P("dp", "ctx", None),
            P("dp", "ctx", None),
            P("dp", "ctx", None),
            P(),
            P("dp", None),
            P("dp", None),
        ),
        check_vma=False,
    )
```

```python
import jax
import jax.numpy as jnp
from jax import lax
from jax.sharding import PartitionSpec as P

SPAN = 256
CH = 3072


eps_norm = 1e-05
clip_norm = 64.0
beta_one = 0.9
beta_two = 0.95
adam_eps = 1e-08
learn_rate = 0.02
step_count = 100.0
highest = lax.Precision.HIGHEST


def to_heads(x, groups):
    _, t, c = x.shape
    x = x.reshape(t, groups, c // groups).transpose(1, 0, 2)
    x = lax.all_to_all(x, "ctx", 0, 0, tiled=True)
    return x.reshape(groups * t, c // groups)


def from_heads(x, groups):
    tw, w = x.shape
    x = x.reshape(groups, tw // groups, w)
    return lax.all_to_all(x, "ctx", 0, 0, tiled=True)


def to_positions(x, groups):
    parts = from_heads(x, groups)
    _, t, w = parts.shape
    return parts.transpose(1, 0, 2).reshape(1, t, groups * w)


def rounded(value):
    return lax.optimization_barrier(value.astype(jnp.bfloat16)).astype(jnp.float32)


def ssd_group(hidden, dt_raw, b_input, c_input, resets, a_log, dt_bias, skip):
    length = hidden.shape[0]
    heads = a_log.shape[0]
    width = hidden.shape[1] // heads
    blocks = length // SPAN
    step_sizes = jax.nn.softplus(dt_raw.astype(jnp.float32) + dt_bias)
    log_decay = (step_sizes * -jnp.exp(a_log)).reshape(blocks, SPAN, heads).transpose(0, 2, 1)
    cumul = jnp.cumsum(log_decay, axis=2)
    inputs = hidden.astype(jnp.float32).reshape(blocks, SPAN, heads, width)
    scaled = rounded(inputs * step_sizes.reshape(blocks, SPAN, heads, 1))
    b_rows = b_input.astype(jnp.float32).reshape(blocks, SPAN, -1)
    c_rows = c_input.astype(jnp.float32).reshape(blocks, SPAN, -1)
    scores = jnp.einsum("ctn,csn->cts", c_rows, b_rows, precision=highest)
    causal = jnp.arange(SPAN)[:, None] >= jnp.arange(SPAN)[None, :]
    spread = cumul[:, :, :, None] - cumul[:, :, None, :]
    decay = jnp.where(causal, jnp.exp(jnp.where(causal, spread, 0.0)), 0.0)
    weights = rounded(scores[:, None] * decay)
    intra = jnp.einsum("chts,cshp->cthp", weights, scaled, precision=highest)
    tail = cumul[:, :, -1:] - cumul
    b_decayed = rounded(b_rows[:, None] * jnp.exp(tail)[..., None])
    block_state = jnp.einsum("chsn,cshp->chnp", b_decayed, scaled, precision=highest)
    keep = 1.0 - resets.astype(jnp.float32)

    def advance(state, items):
        keep_one, total, added = items
        entering = state * keep_one
        return (jnp.exp(total)[:, None, None] * entering + added, entering)

    start_state = jnp.zeros(block_state.shape[1:], jnp.float32)
    last_state, entering = lax.scan(advance, start_state, (keep, cumul[:, :, -1], block_state))
    c_decayed = rounded(c_rows[:, None] * jnp.exp(cumul)[..., None])
    inter = jnp.einsum("chtn,chnp->cthp", c_decayed, rounded(entering), precision=highest)
    output = intra + inter + skip[:, None] * inputs
    return output.reshape(length, heads * width).astype(jnp.bfloat16)


def gate_values(y_values, gating):
    gated = y_values.astype(jnp.float32) * jax.nn.silu(gating.astype(jnp.float32))
    return (gated, jnp.sum(gated * gated, axis=-1))


def normalize(gated, total, gain):
    factor = lax.rsqrt(total / CH + eps_norm)
    return (factor, (gated * factor[..., None] * gain).astype(jnp.bfloat16))


def norm_backward(cotangent, gain, gated, factor, dot_total, y_values, gating):
    upstream = cotangent.astype(jnp.float32) * gain
    d_gated = (
        upstream * factor[..., None]
        - gated * (factor * factor * factor * dot_total / CH)[..., None]
    )
    gate_f = gating.astype(jnp.float32)
    sigma = jax.nn.sigmoid(gate_f)
    d_y = (d_gated * (gate_f * sigma)).astype(jnp.bfloat16)
    d_gate = (
        d_gated * y_values.astype(jnp.float32) * sigma * (1.0 + gate_f * (1.0 - sigma))
    ).astype(jnp.bfloat16)
    d_gain = jnp.sum(
        cotangent.astype(jnp.float32) * gated * factor[..., None], axis=tuple(range(gated.ndim - 1))
    )
    return (d_y, d_gate, d_gain)


def on_device(
    hidden,
    gating,
    dt_raw,
    b_input,
    c_input,
    resets,
    cotangent,
    parameters,
    adam_mean,
    adam_square,
    bucket_size,
    bucket_owner,
):
    heads_all = dt_raw.shape[2]
    groups = lax.axis_size("ctx")
    group = heads_all // groups
    state_size = b_input.shape[2]
    tokens = hidden.shape[1]
    first = lax.axis_index("ctx") * group
    head_params = parameters[: 3 * heads_all].reshape(3, heads_all)
    gain = parameters[3 * heads_all :]
    local_params = lax.dynamic_slice_in_dim(head_params, first, group, 1)
    bc_all = lax.all_gather(jnp.concatenate([b_input, c_input], axis=2), "ctx", axis=1, tiled=True)
    b_all = bc_all[..., :state_size]
    c_all = bc_all[..., state_size:]
    seq_resets = resets[0]
    owners_n = lax.axis_size("dp")
    cap_n = adam_mean.shape[1]
    len_n = parameters.shape[0]
    state_all = lax.all_gather(jnp.stack([adam_mean[0], adam_square[0]]), "dp", axis=0)
    starts = jnp.cumsum(bucket_size) - bucket_size
    laid = jnp.zeros((2, len_n + cap_n), jnp.float32)
    for k in range(owners_n):
        laid = lax.dynamic_update_slice(laid, state_all[bucket_owner[k]], (0, starts[k]))
    mean_flat = laid[0, :len_n]
    square_flat = laid[1, :len_n]

    def local_fn(x_arg, dt_arg, b_arg, c_arg, a_arg, bias_arg, skip_arg):
        return ssd_group(x_arg, dt_arg, b_arg, c_arg, seq_resets, a_arg, bias_arg, skip_arg)

    x_heads, dt_heads = (
        to_heads(hidden, groups)[None],
        to_heads(dt_raw, groups)[None],
    )
    y_heads, pullback = jax.vjp(
        local_fn,
        x_heads[0],
        dt_heads[0],
        b_all[0],
        c_all[0],
        local_params[0],
        local_params[1],
        local_params[2],
    )
    y_seq = to_positions(y_heads, groups)
    gated, total = gate_values(y_seq, gating)
    factor, normed = normalize(gated, total, gain)
    dot_total = jnp.sum(cotangent.astype(jnp.float32) * gain * gated, axis=-1)
    d_y, grad_gating, d_gain = norm_backward(
        cotangent, gain, gated, factor, dot_total, y_seq, gating
    )
    d_y_heads = to_heads(d_y, groups)[None]
    d_x, d_dt, d_b, d_c, d_alog, d_bias, d_skip = pullback(d_y_heads[0])
    d_pair = jnp.concatenate([d_b, d_c], axis=-1)
    grad_hidden, grad_dt, pair_parts = (
        to_positions(d_x, groups),
        to_positions(d_dt, groups),
        from_heads(d_pair, groups),
    )
    pair_sum = jnp.sum(pair_parts.astype(jnp.float32), axis=0)[None].astype(jnp.bfloat16)
    grad_b = pair_sum[..., :state_size]
    grad_c = pair_sum[..., state_size:]
    head_grads = jnp.stack([d_alog, d_bias, d_skip])
    full_heads = lax.dynamic_update_slice(
        jnp.zeros((3, heads_all), jnp.float32), head_grads, (0, first)
    )
    grad_part = jnp.concatenate([full_heads.reshape(-1), d_gain])
    gradient = lax.psum(grad_part, ("dp", "ctx"))
    grad_norm = jnp.sqrt(jnp.sum(gradient * gradient))
    shrink = jnp.minimum(1.0, clip_norm / (grad_norm + 1e-06))
    owners = lax.axis_size("dp")
    slot_cap = adam_mean.shape[1]
    total_len = parameters.shape[0]
    ends = jnp.cumsum(bucket_size)
    begins = ends - bucket_size
    order = jnp.arange(owners, dtype=jnp.int32)
    mine = lax.axis_index("dp")
    my_bucket = jnp.sum(jnp.where(bucket_owner == mine, order, 0))
    row_begin = jnp.sum(jnp.where(order == my_bucket, begins, 0))
    row_size = jnp.sum(jnp.where(order == my_bucket, bucket_size, 0))
    slots = jnp.arange(slot_cap, dtype=jnp.int32)
    valid = slots < row_size
    padding = jnp.zeros((slot_cap,), jnp.float32)
    grad_row = (
        jnp.where(
            valid,
            lax.dynamic_slice_in_dim(jnp.concatenate([gradient, padding]), row_begin, slot_cap),
            0.0,
        )
        * shrink
    )
    new_mean = beta_one * adam_mean[0] + (1.0 - beta_one) * grad_row
    new_square = beta_two * adam_square[0] + (1.0 - beta_two) * grad_row * grad_row
    grad_flat = gradient * shrink
    mean_all = beta_one * mean_flat + (1.0 - beta_one) * grad_flat
    square_all = beta_two * square_flat + (1.0 - beta_two) * grad_flat * grad_flat
    direction = (
        mean_all
        / (1.0 - beta_one**step_count)
        / (jnp.sqrt(square_all / (1.0 - beta_two**step_count)) + adam_eps)
    )
    new_params = parameters - learn_rate * direction
    return (
        normed,
        grad_hidden,
        grad_gating,
        grad_dt,
        grad_b,
        grad_c,
        new_params,
        new_mean[None],
        new_square[None],
    )


def solution(mesh):
    return jax.shard_map(
        on_device,
        mesh=mesh,
        in_specs=(
            P("dp", "ctx", None),
            P("dp", "ctx", None),
            P("dp", "ctx", None),
            P("dp", "ctx", None),
            P("dp", "ctx", None),
            P("dp", None),
            P("dp", "ctx", None),
            P(),
            P("dp", None),
            P("dp", None),
            P(),
            P(),
        ),
        out_specs=(
            P("dp", "ctx", None),
            P("dp", "ctx", None),
            P("dp", "ctx", None),
            P("dp", "ctx", None),
            P("dp", "ctx", None),
            P("dp", "ctx", None),
            P(),
            P("dp", None),
            P("dp", None),
        ),
        check_vma=False,
    )
```

```python
import jax
import jax.numpy as jnp
from jax import lax
from jax.sharding import PartitionSpec as P

SPAN = 256
CH = 3072


eps_norm = 1e-05
clip_norm = 64.0
beta_one = 0.9
beta_two = 0.95
adam_eps = 1e-08
learn_rate = 0.02
step_count = 100.0
highest = lax.Precision.HIGHEST


def to_heads(x, groups):
    _, t, c = x.shape
    x = x.reshape(t, groups, c // groups).transpose(1, 0, 2)
    x = lax.all_to_all(x, "ctx", 0, 0, tiled=True)
    return x.reshape(groups * t, c // groups)


def from_heads(x, groups):
    tw, w = x.shape
    x = x.reshape(groups, tw // groups, w)
    return lax.all_to_all(x, "ctx", 0, 0, tiled=True)


def to_positions(x, groups):
    parts = from_heads(x, groups)
    _, t, w = parts.shape
    return parts.transpose(1, 0, 2).reshape(1, t, groups * w)


def tree_sum(x, axis):
    size = lax.axis_size(axis)
    if size & (size - 1):
        return lax.psum(x, axis)
    step = 1
    while step < size:
        x = x + lax.ppermute(x, axis, [(i, i ^ step) for i in range(size)])
        step *= 2
    return x


def rounded(value):
    return lax.optimization_barrier(value.astype(jnp.bfloat16)).astype(jnp.float32)


def ssd_group(hidden, dt_raw, b_input, c_input, resets, a_log, dt_bias, skip):
    length = hidden.shape[0]
    heads = a_log.shape[0]
    width = hidden.shape[1] // heads
    blocks = length // SPAN
    step_sizes = jax.nn.softplus(dt_raw.astype(jnp.float32) + dt_bias)
    log_decay = (step_sizes * -jnp.exp(a_log)).reshape(blocks, SPAN, heads).transpose(0, 2, 1)
    cumul = jnp.cumsum(log_decay, axis=2)
    inputs = hidden.astype(jnp.float32).reshape(blocks, SPAN, heads, width)
    scaled = rounded(inputs * step_sizes.reshape(blocks, SPAN, heads, 1))
    b_rows = b_input.astype(jnp.float32).reshape(blocks, SPAN, -1)
    c_rows = c_input.astype(jnp.float32).reshape(blocks, SPAN, -1)
    scores = jnp.einsum("ctn,csn->cts", c_rows, b_rows, precision=highest)
    causal = jnp.arange(SPAN)[:, None] >= jnp.arange(SPAN)[None, :]
    spread = cumul[:, :, :, None] - cumul[:, :, None, :]
    decay = jnp.where(causal, jnp.exp(jnp.where(causal, spread, 0.0)), 0.0)
    weights = rounded(scores[:, None] * decay)
    intra = jnp.einsum("chts,cshp->cthp", weights, scaled, precision=highest)
    tail = cumul[:, :, -1:] - cumul
    b_decayed = rounded(b_rows[:, None] * jnp.exp(tail)[..., None])
    block_state = jnp.einsum("chsn,cshp->chnp", b_decayed, scaled, precision=highest)
    keep = 1.0 - resets.astype(jnp.float32)

    def advance(state, items):
        keep_one, total, added = items
        entering = state * keep_one
        return (jnp.exp(total)[:, None, None] * entering + added, entering)

    start_state = jnp.zeros(block_state.shape[1:], jnp.float32)
    last_state, entering = lax.scan(advance, start_state, (keep, cumul[:, :, -1], block_state))
    c_decayed = rounded(c_rows[:, None] * jnp.exp(cumul)[..., None])
    inter = jnp.einsum("chtn,chnp->cthp", c_decayed, rounded(entering), precision=highest)
    output = intra + inter + skip[:, None] * inputs
    return output.reshape(length, heads * width).astype(jnp.bfloat16)


def gate_values(y_values, gating):
    gated = y_values.astype(jnp.float32) * jax.nn.silu(gating.astype(jnp.float32))
    return (gated, jnp.sum(gated * gated, axis=-1))


def normalize(gated, total, gain):
    factor = lax.rsqrt(total / CH + eps_norm)
    return (factor, (gated * factor[..., None] * gain).astype(jnp.bfloat16))


def norm_backward(cotangent, gain, gated, factor, dot_total, y_values, gating):
    upstream = cotangent.astype(jnp.float32) * gain
    d_gated = (
        upstream * factor[..., None]
        - gated * (factor * factor * factor * dot_total / CH)[..., None]
    )
    gate_f = gating.astype(jnp.float32)
    sigma = jax.nn.sigmoid(gate_f)
    d_y = (d_gated * (gate_f * sigma)).astype(jnp.bfloat16)
    d_gate = (
        d_gated * y_values.astype(jnp.float32) * sigma * (1.0 + gate_f * (1.0 - sigma))
    ).astype(jnp.bfloat16)
    d_gain = jnp.sum(
        cotangent.astype(jnp.float32) * gated * factor[..., None], axis=tuple(range(gated.ndim - 1))
    )
    return (d_y, d_gate, d_gain)


def on_device(
    hidden,
    gating,
    dt_raw,
    b_input,
    c_input,
    resets,
    cotangent,
    parameters,
    adam_mean,
    adam_square,
    bucket_size,
    bucket_owner,
):
    heads_all = dt_raw.shape[2]
    groups = lax.axis_size("ctx")
    group = heads_all // groups
    state_size = b_input.shape[2]
    tokens = hidden.shape[1]
    first = lax.axis_index("ctx") * group
    head_params = parameters[: 3 * heads_all].reshape(3, heads_all)
    gain = parameters[3 * heads_all :]
    local_params = lax.dynamic_slice_in_dim(head_params, first, group, 1)
    bc_all = lax.all_gather(jnp.concatenate([b_input, c_input], axis=2), "ctx", axis=1, tiled=True)
    b_all = bc_all[..., :state_size]
    c_all = bc_all[..., state_size:]
    seq_resets = resets[0]

    def local_fn(x_arg, dt_arg, b_arg, c_arg, a_arg, bias_arg, skip_arg):
        return ssd_group(x_arg, dt_arg, b_arg, c_arg, seq_resets, a_arg, bias_arg, skip_arg)

    x_heads, dt_heads = (
        to_heads(hidden, groups)[None],
        to_heads(dt_raw, groups)[None],
    )
    y_heads, pullback = jax.vjp(
        local_fn,
        x_heads[0],
        dt_heads[0],
        b_all[0],
        c_all[0],
        local_params[0],
        local_params[1],
        local_params[2],
    )
    y_seq = to_positions(y_heads, groups)
    gated, total = gate_values(y_seq, gating)
    factor, normed = normalize(gated, total, gain)
    dot_total = jnp.sum(cotangent.astype(jnp.float32) * gain * gated, axis=-1)
    d_y, grad_gating, d_gain = norm_backward(
        cotangent, gain, gated, factor, dot_total, y_seq, gating
    )
    d_y_heads = to_heads(d_y, groups)[None]
    d_x, d_dt, d_b, d_c, d_alog, d_bias, d_skip = pullback(d_y_heads[0])
    d_pair = jnp.concatenate([d_b, d_c], axis=-1)
    grad_hidden, grad_dt, pair_parts = (
        to_positions(d_x, groups),
        to_positions(d_dt, groups),
        from_heads(d_pair, groups),
    )
    pair_sum = jnp.sum(pair_parts.astype(jnp.float32), axis=0)[None].astype(jnp.bfloat16)
    grad_b = pair_sum[..., :state_size]
    grad_c = pair_sum[..., state_size:]
    head_grads = jnp.stack([d_alog, d_bias, d_skip])
    full_heads = lax.dynamic_update_slice(
        jnp.zeros((3, heads_all), jnp.float32), head_grads, (0, first)
    )
    grad_part = jnp.concatenate([full_heads.reshape(-1), d_gain])
    owners = lax.axis_size("dp")
    slot_cap = adam_mean.shape[1]
    total_len = parameters.shape[0]
    ends = jnp.cumsum(bucket_size)
    begins = ends - bucket_size
    order = jnp.arange(owners, dtype=jnp.int32)
    mine = lax.axis_index("dp")
    my_bucket = jnp.sum(jnp.where(bucket_owner == mine, order, 0))
    row_begin = jnp.sum(jnp.where(order == my_bucket, begins, 0))
    row_size = jnp.sum(jnp.where(order == my_bucket, bucket_size, 0))
    slots = jnp.arange(slot_cap, dtype=jnp.int32)
    valid = slots < row_size
    padding = jnp.zeros((slot_cap,), jnp.float32)
    sender = (lax.axis_index("ctx") == 0) & valid
    own_state = jnp.where(sender, jnp.stack([adam_mean[0], adam_square[0]]), 0.0)
    laid = lax.dynamic_update_slice(
        jnp.zeros((2, total_len + slot_cap), jnp.float32), own_state, (0, row_begin)
    )[:, :total_len]
    summed = tree_sum(tree_sum(jnp.concatenate([grad_part[None], laid]), "ctx"), "dp")
    gradient = summed[0]
    mean_flat = summed[1]
    square_flat = summed[2]
    grad_norm = jnp.sqrt(jnp.sum(gradient * gradient))
    shrink = jnp.minimum(1.0, clip_norm / (grad_norm + 1e-06))
    grad_row = (
        jnp.where(
            valid,
            lax.dynamic_slice_in_dim(jnp.concatenate([gradient, padding]), row_begin, slot_cap),
            0.0,
        )
        * shrink
    )
    new_mean = beta_one * adam_mean[0] + (1.0 - beta_one) * grad_row
    new_square = beta_two * adam_square[0] + (1.0 - beta_two) * grad_row * grad_row
    grad_flat = gradient * shrink
    mean_all = beta_one * mean_flat + (1.0 - beta_one) * grad_flat
    square_all = beta_two * square_flat + (1.0 - beta_two) * grad_flat * grad_flat
    direction = (
        mean_all
        / (1.0 - beta_one**step_count)
        / (jnp.sqrt(square_all / (1.0 - beta_two**step_count)) + adam_eps)
    )
    new_params = parameters - learn_rate * direction
    return (
        normed,
        grad_hidden,
        grad_gating,
        grad_dt,
        grad_b,
        grad_c,
        new_params,
        new_mean[None],
        new_square[None],
    )


def solution(mesh):
    return jax.shard_map(
        on_device,
        mesh=mesh,
        in_specs=(
            P("dp", "ctx", None),
            P("dp", "ctx", None),
            P("dp", "ctx", None),
            P("dp", "ctx", None),
            P("dp", "ctx", None),
            P("dp", None),
            P("dp", "ctx", None),
            P(),
            P("dp", None),
            P("dp", None),
            P(),
            P(),
        ),
        out_specs=(
            P("dp", "ctx", None),
            P("dp", "ctx", None),
            P("dp", "ctx", None),
            P("dp", "ctx", None),
            P("dp", "ctx", None),
            P("dp", "ctx", None),
            P(),
            P("dp", None),
            P("dp", None),
        ),
        check_vma=False,
    )
```

```python
import jax
import jax.numpy as jnp
from jax import lax
from jax.sharding import PartitionSpec as P

SPAN = 256
CH = 3072


eps_norm = 1e-05
clip_norm = 64.0
beta_one = 0.9
beta_two = 0.95
adam_eps = 1e-08
learn_rate = 0.02
step_count = 100.0
highest = lax.Precision.HIGHEST


def to_heads(x, groups):
    _, t, c = x.shape
    x = x.reshape(t, groups, c // groups).transpose(1, 0, 2)
    x = lax.all_to_all(x, "ctx", 0, 0, tiled=True)
    return x.reshape(groups * t, c // groups)


def from_heads(x, groups):
    tw, w = x.shape
    x = x.reshape(groups, tw // groups, w)
    return lax.all_to_all(x, "ctx", 0, 0, tiled=True)


def to_positions(x, groups):
    parts = from_heads(x, groups)
    _, t, w = parts.shape
    return parts.transpose(1, 0, 2).reshape(1, t, groups * w)


def tree_sum(x, axis):
    size = lax.axis_size(axis)
    if size & (size - 1):
        return lax.psum(x, axis)
    step = 1
    while step < size:
        x = x + lax.ppermute(x, axis, [(i, i ^ step) for i in range(size)])
        step *= 2
    return x


def rounded(value):
    return lax.optimization_barrier(value.astype(jnp.bfloat16)).astype(jnp.float32)


def ssd_group(hidden, dt_raw, b_input, c_input, resets, a_log, dt_bias, skip):
    length = hidden.shape[0]
    heads = a_log.shape[0]
    width = hidden.shape[1] // heads
    blocks = length // SPAN
    step_sizes = jax.nn.softplus(dt_raw.astype(jnp.float32) + dt_bias)
    log_decay = (step_sizes * -jnp.exp(a_log)).reshape(blocks, SPAN, heads).transpose(0, 2, 1)
    cumul = jnp.cumsum(log_decay, axis=2)
    inputs = hidden.astype(jnp.float32).reshape(blocks, SPAN, heads, width)
    scaled = rounded(inputs * step_sizes.reshape(blocks, SPAN, heads, 1))
    b_rows = b_input.astype(jnp.float32).reshape(blocks, SPAN, -1)
    c_rows = c_input.astype(jnp.float32).reshape(blocks, SPAN, -1)
    scores = jnp.einsum("ctn,csn->cts", c_rows, b_rows, precision=highest)
    causal = jnp.arange(SPAN)[:, None] >= jnp.arange(SPAN)[None, :]
    spread = cumul[:, :, :, None] - cumul[:, :, None, :]
    decay = jnp.where(causal, jnp.exp(jnp.where(causal, spread, 0.0)), 0.0)
    weights = rounded(scores[:, None] * decay)
    intra = jnp.einsum("chts,cshp->cthp", weights, scaled, precision=highest)
    tail = cumul[:, :, -1:] - cumul
    b_decayed = rounded(b_rows[:, None] * jnp.exp(tail)[..., None])
    block_state = jnp.einsum("chsn,cshp->chnp", b_decayed, scaled, precision=highest)
    keep = 1.0 - resets.astype(jnp.float32)

    def advance(state, items):
        keep_one, total, added = items
        entering = state * keep_one
        return (jnp.exp(total)[:, None, None] * entering + added, entering)

    start_state = jnp.zeros(block_state.shape[1:], jnp.float32)
    last_state, entering = lax.scan(advance, start_state, (keep, cumul[:, :, -1], block_state))
    c_decayed = rounded(c_rows[:, None] * jnp.exp(cumul)[..., None])
    inter = jnp.einsum("chtn,chnp->cthp", c_decayed, rounded(entering), precision=highest)
    output = intra + inter + skip[:, None] * inputs
    return output.reshape(length, heads * width).astype(jnp.bfloat16)


def gate_values(y_values, gating):
    gated = y_values.astype(jnp.float32) * jax.nn.silu(gating.astype(jnp.float32))
    return (gated, jnp.sum(gated * gated, axis=-1))


def normalize(gated, total, gain):
    factor = lax.rsqrt(total / CH + eps_norm)
    return (factor, (gated * factor[..., None] * gain).astype(jnp.bfloat16))


def norm_backward(cotangent, gain, gated, factor, dot_total, y_values, gating):
    upstream = cotangent.astype(jnp.float32) * gain
    d_gated = (
        upstream * factor[..., None]
        - gated * (factor * factor * factor * dot_total / CH)[..., None]
    )
    gate_f = gating.astype(jnp.float32)
    sigma = jax.nn.sigmoid(gate_f)
    d_y = (d_gated * (gate_f * sigma)).astype(jnp.bfloat16)
    d_gate = (
        d_gated * y_values.astype(jnp.float32) * sigma * (1.0 + gate_f * (1.0 - sigma))
    ).astype(jnp.bfloat16)
    d_gain = jnp.sum(
        cotangent.astype(jnp.float32) * gated * factor[..., None], axis=tuple(range(gated.ndim - 1))
    )
    return (d_y, d_gate, d_gain)


def on_device(
    hidden,
    gating,
    dt_raw,
    b_input,
    c_input,
    resets,
    cotangent,
    parameters,
    adam_mean,
    adam_square,
    bucket_size,
    bucket_owner,
):
    heads_all = dt_raw.shape[2]
    groups = lax.axis_size("ctx")
    group = heads_all // groups
    state_size = b_input.shape[2]
    tokens = hidden.shape[1]
    first = lax.axis_index("ctx") * group
    head_params = parameters[: 3 * heads_all].reshape(3, heads_all)
    gain = parameters[3 * heads_all :]
    local_params = lax.dynamic_slice_in_dim(head_params, first, group, 1)
    width = hidden.shape[2] // groups
    shared = jnp.concatenate([b_input[0], c_input[0]], axis=1)
    packed = jnp.concatenate(
        [
            hidden[0].reshape(tokens, groups, width).transpose(1, 0, 2),
            jnp.broadcast_to(shared[None], (groups,) + shared.shape),
            dt_raw[0].reshape(tokens, groups, group).transpose(1, 0, 2),
        ],
        axis=2,
    )
    arrived = lax.all_to_all(packed, "ctx", 0, 0, tiled=True).reshape(groups * tokens, -1)
    b_all = arrived[None, :, width : width + state_size]
    c_all = arrived[None, :, width + state_size : width + 2 * state_size]
    seq_resets = resets[0]

    def local_fn(x_arg, dt_arg, b_arg, c_arg, a_arg, bias_arg, skip_arg):
        return ssd_group(x_arg, dt_arg, b_arg, c_arg, seq_resets, a_arg, bias_arg, skip_arg)

    x_heads = arrived[None, :, :width]
    dt_heads = arrived[None, :, width + 2 * state_size :]
    y_heads, pullback = jax.vjp(
        local_fn,
        x_heads[0],
        dt_heads[0],
        b_all[0],
        c_all[0],
        local_params[0],
        local_params[1],
        local_params[2],
    )
    y_seq = to_positions(y_heads, groups)
    gated, total = gate_values(y_seq, gating)
    factor, normed = normalize(gated, total, gain)
    dot_total = jnp.sum(cotangent.astype(jnp.float32) * gain * gated, axis=-1)
    d_y, grad_gating, d_gain = norm_backward(
        cotangent, gain, gated, factor, dot_total, y_seq, gating
    )
    d_y_heads = to_heads(d_y, groups)[None]
    d_x, d_dt, d_b, d_c, d_alog, d_bias, d_skip = pullback(d_y_heads[0])
    back = from_heads(jnp.concatenate([d_x, d_b, d_c, d_dt], axis=-1), groups)
    grad_hidden = back[..., :width].transpose(1, 0, 2).reshape(1, tokens, groups * width)
    grad_dt = back[..., width + 2 * state_size :].transpose(1, 0, 2).reshape(1, tokens, heads_all)
    pair_sum = jnp.sum(
        back[..., width : width + 2 * state_size].astype(jnp.float32), axis=0
    )[None].astype(jnp.bfloat16)
    grad_b = pair_sum[..., :state_size]
    grad_c = pair_sum[..., state_size:]
    head_grads = jnp.stack([d_alog, d_bias, d_skip])
    full_heads = lax.dynamic_update_slice(
        jnp.zeros((3, heads_all), jnp.float32), head_grads, (0, first)
    )
    grad_part = jnp.concatenate([full_heads.reshape(-1), d_gain])
    owners = lax.axis_size("dp")
    slot_cap = adam_mean.shape[1]
    total_len = parameters.shape[0]
    ends = jnp.cumsum(bucket_size)
    begins = ends - bucket_size
    order = jnp.arange(owners, dtype=jnp.int32)
    mine = lax.axis_index("dp")
    my_bucket = jnp.sum(jnp.where(bucket_owner == mine, order, 0))
    row_begin = jnp.sum(jnp.where(order == my_bucket, begins, 0))
    row_size = jnp.sum(jnp.where(order == my_bucket, bucket_size, 0))
    slots = jnp.arange(slot_cap, dtype=jnp.int32)
    valid = slots < row_size
    padding = jnp.zeros((slot_cap,), jnp.float32)
    sender = (lax.axis_index("ctx") == 0) & valid
    own_state = jnp.where(sender, jnp.stack([adam_mean[0], adam_square[0]]), 0.0)
    laid = lax.dynamic_update_slice(
        jnp.zeros((2, total_len + slot_cap), jnp.float32), own_state, (0, row_begin)
    )[:, :total_len]
    summed = tree_sum(tree_sum(jnp.concatenate([grad_part[None], laid]), "ctx"), "dp")
    gradient = summed[0]
    mean_flat = summed[1]
    square_flat = summed[2]
    grad_norm = jnp.sqrt(jnp.sum(gradient * gradient))
    shrink = jnp.minimum(1.0, clip_norm / (grad_norm + 1e-06))
    grad_row = (
        jnp.where(
            valid,
            lax.dynamic_slice_in_dim(jnp.concatenate([gradient, padding]), row_begin, slot_cap),
            0.0,
        )
        * shrink
    )
    new_mean = beta_one * adam_mean[0] + (1.0 - beta_one) * grad_row
    new_square = beta_two * adam_square[0] + (1.0 - beta_two) * grad_row * grad_row
    grad_flat = gradient * shrink
    mean_all = beta_one * mean_flat + (1.0 - beta_one) * grad_flat
    square_all = beta_two * square_flat + (1.0 - beta_two) * grad_flat * grad_flat
    direction = (
        mean_all
        / (1.0 - beta_one**step_count)
        / (jnp.sqrt(square_all / (1.0 - beta_two**step_count)) + adam_eps)
    )
    new_params = parameters - learn_rate * direction
    return (
        normed,
        grad_hidden,
        grad_gating,
        grad_dt,
        grad_b,
        grad_c,
        new_params,
        new_mean[None],
        new_square[None],
    )


def solution(mesh):
    return jax.shard_map(
        on_device,
        mesh=mesh,
        in_specs=(
            P("dp", "ctx", None),
            P("dp", "ctx", None),
            P("dp", "ctx", None),
            P("dp", "ctx", None),
            P("dp", "ctx", None),
            P("dp", None),
            P("dp", "ctx", None),
            P(),
            P("dp", None),
            P("dp", None),
            P(),
            P(),
        ),
        out_specs=(
            P("dp", "ctx", None),
            P("dp", "ctx", None),
            P("dp", "ctx", None),
            P("dp", "ctx", None),
            P("dp", "ctx", None),
            P("dp", "ctx", None),
            P(),
            P("dp", None),
            P("dp", None),
        ),
        check_vma=False,
    )
```

```python
import jax
import jax.numpy as jnp
from jax import lax
from jax.sharding import PartitionSpec as P

SPAN = 256
CH = 3072


eps_norm = 1e-05
clip_norm = 64.0
beta_one = 0.9
beta_two = 0.95
adam_eps = 1e-08
learn_rate = 0.02
step_count = 100.0
highest = lax.Precision.HIGHEST


def to_heads(x, groups):
    _, t, c = x.shape
    x = x.reshape(t, groups, c // groups).transpose(1, 0, 2)
    x = lax.all_to_all(x, "ctx", 0, 0, tiled=True)
    return x.reshape(groups * t, c // groups)


def from_heads(x, groups):
    tw, w = x.shape
    x = x.reshape(groups, tw // groups, w)
    return lax.all_to_all(x, "ctx", 0, 0, tiled=True)


def to_positions(x, groups):
    parts = from_heads(x, groups)
    _, t, w = parts.shape
    return parts.transpose(1, 0, 2).reshape(1, t, groups * w)


def tree_sum(x, axis):
    size = lax.axis_size(axis)
    if size & (size - 1):
        return lax.psum(x, axis)
    step = 1
    while step < size:
        x = x + lax.ppermute(x, axis, [(i, i ^ step) for i in range(size)])
        step *= 2
    return x


def rounded(value):
    return lax.optimization_barrier(value.astype(jnp.bfloat16)).astype(jnp.float32)


def ssd_group(hidden, dt_raw, b_input, c_input, resets, a_log, dt_bias, skip):
    length = hidden.shape[0]
    heads = a_log.shape[0]
    width = hidden.shape[1] // heads
    blocks = length // SPAN
    step_sizes = jax.nn.softplus(dt_raw.astype(jnp.float32) + dt_bias)
    log_decay = (step_sizes * -jnp.exp(a_log)).reshape(blocks, SPAN, heads).transpose(0, 2, 1)
    lower = (jnp.arange(SPAN)[:, None] >= jnp.arange(SPAN)[None, :]).astype(jnp.float32)
    cumul = jnp.einsum("chs,ts->cht", log_decay, lower, precision=highest)
    inputs = hidden.astype(jnp.float32).reshape(blocks, SPAN, heads, width)
    scaled = rounded(inputs * step_sizes.reshape(blocks, SPAN, heads, 1))
    b_rows = b_input.astype(jnp.float32).reshape(blocks, SPAN, -1)
    c_rows = c_input.astype(jnp.float32).reshape(blocks, SPAN, -1)
    scores = jnp.einsum("ctn,csn->cts", c_rows, b_rows, precision=highest)
    causal = jnp.arange(SPAN)[:, None] >= jnp.arange(SPAN)[None, :]
    spread = cumul[:, :, :, None] - cumul[:, :, None, :]
    decay = jnp.where(causal, jnp.exp(jnp.where(causal, spread, 0.0)), 0.0)
    weights = rounded(scores[:, None] * decay)
    intra = jnp.einsum("chts,cshp->cthp", weights, scaled, precision=highest)
    tail = cumul[:, :, -1:] - cumul
    b_decayed = rounded(b_rows[:, None] * jnp.exp(tail)[..., None])
    block_state = jnp.einsum("chsn,cshp->chnp", b_decayed, scaled, precision=highest)
    keep = 1.0 - resets.astype(jnp.float32)

    def advance(state, items):
        keep_one, total, added = items
        entering = state * keep_one
        return (jnp.exp(total)[:, None, None] * entering + added, entering)

    start_state = jnp.zeros(block_state.shape[1:], jnp.float32)
    last_state, entering = lax.scan(
        advance, start_state, (keep, cumul[:, :, -1], block_state), unroll=True
    )
    c_decayed = rounded(c_rows[:, None] * jnp.exp(cumul)[..., None])
    inter = jnp.einsum("chtn,chnp->cthp", c_decayed, rounded(entering), precision=highest)
    output = intra + inter + skip[:, None] * inputs
    return output.reshape(length, heads * width).astype(jnp.bfloat16)


def gate_values(y_values, gating):
    gated = y_values.astype(jnp.float32) * jax.nn.silu(gating.astype(jnp.float32))
    return (gated, jnp.sum(gated * gated, axis=-1))


def normalize(gated, total, gain):
    factor = lax.rsqrt(total / CH + eps_norm)
    return (factor, (gated * factor[..., None] * gain).astype(jnp.bfloat16))


def norm_backward(cotangent, gain, gated, factor, dot_total, y_values, gating):
    upstream = cotangent.astype(jnp.float32) * gain
    d_gated = (
        upstream * factor[..., None]
        - gated * (factor * factor * factor * dot_total / CH)[..., None]
    )
    gate_f = gating.astype(jnp.float32)
    sigma = jax.nn.sigmoid(gate_f)
    d_y = (d_gated * (gate_f * sigma)).astype(jnp.bfloat16)
    d_gate = (
        d_gated * y_values.astype(jnp.float32) * sigma * (1.0 + gate_f * (1.0 - sigma))
    ).astype(jnp.bfloat16)
    d_gain = jnp.sum(
        cotangent.astype(jnp.float32) * gated * factor[..., None], axis=tuple(range(gated.ndim - 1))
    )
    return (d_y, d_gate, d_gain)


def on_device(
    hidden,
    gating,
    dt_raw,
    b_input,
    c_input,
    resets,
    cotangent,
    parameters,
    adam_mean,
    adam_square,
    bucket_size,
    bucket_owner,
):
    heads_all = dt_raw.shape[2]
    groups = lax.axis_size("ctx")
    group = heads_all // groups
    state_size = b_input.shape[2]
    tokens = hidden.shape[1]
    first = lax.axis_index("ctx") * group
    head_params = parameters[: 3 * heads_all].reshape(3, heads_all)
    gain = parameters[3 * heads_all :]
    local_params = lax.dynamic_slice_in_dim(head_params, first, group, 1)
    width = hidden.shape[2] // groups
    shared = jnp.concatenate([b_input[0], c_input[0]], axis=1)
    packed = jnp.concatenate(
        [
            hidden[0].reshape(tokens, groups, width).transpose(1, 0, 2),
            jnp.broadcast_to(shared[None], (groups,) + shared.shape),
            dt_raw[0].reshape(tokens, groups, group).transpose(1, 0, 2),
        ],
        axis=2,
    )
    arrived = lax.all_to_all(packed, "ctx", 0, 0, tiled=True).reshape(groups * tokens, -1)
    b_all = arrived[None, :, width : width + state_size]
    c_all = arrived[None, :, width + state_size : width + 2 * state_size]
    seq_resets = resets[0]

    def local_fn(x_arg, dt_arg, b_arg, c_arg, a_arg, bias_arg, skip_arg):
        return ssd_group(x_arg, dt_arg, b_arg, c_arg, seq_resets, a_arg, bias_arg, skip_arg)

    x_heads = arrived[None, :, :width]
    dt_heads = arrived[None, :, width + 2 * state_size :]
    y_heads, pullback = jax.vjp(
        local_fn,
        x_heads[0],
        dt_heads[0],
        b_all[0],
        c_all[0],
        local_params[0],
        local_params[1],
        local_params[2],
    )
    y_seq = to_positions(y_heads, groups)
    gated, total = gate_values(y_seq, gating)
    factor, normed = normalize(gated, total, gain)
    dot_total = jnp.sum(cotangent.astype(jnp.float32) * gain * gated, axis=-1)
    d_y, grad_gating, d_gain = norm_backward(
        cotangent, gain, gated, factor, dot_total, y_seq, gating
    )
    d_y_heads = to_heads(d_y, groups)[None]
    d_x, d_dt, d_b, d_c, d_alog, d_bias, d_skip = pullback(d_y_heads[0])
    back = from_heads(jnp.concatenate([d_x, d_b, d_c, d_dt], axis=-1), groups)
    grad_hidden = back[..., :width].transpose(1, 0, 2).reshape(1, tokens, groups * width)
    grad_dt = back[..., width + 2 * state_size :].transpose(1, 0, 2).reshape(1, tokens, heads_all)
    pair_sum = jnp.sum(
        back[..., width : width + 2 * state_size].astype(jnp.float32), axis=0
    )[None].astype(jnp.bfloat16)
    grad_b = pair_sum[..., :state_size]
    grad_c = pair_sum[..., state_size:]
    head_grads = jnp.stack([d_alog, d_bias, d_skip])
    full_heads = lax.dynamic_update_slice(
        jnp.zeros((3, heads_all), jnp.float32), head_grads, (0, first)
    )
    grad_part = jnp.concatenate([full_heads.reshape(-1), d_gain])
    owners = lax.axis_size("dp")
    slot_cap = adam_mean.shape[1]
    total_len = parameters.shape[0]
    ends = jnp.cumsum(bucket_size)
    begins = ends - bucket_size
    order = jnp.arange(owners, dtype=jnp.int32)
    mine = lax.axis_index("dp")
    my_bucket = jnp.sum(jnp.where(bucket_owner == mine, order, 0))
    row_begin = jnp.sum(jnp.where(order == my_bucket, begins, 0))
    row_size = jnp.sum(jnp.where(order == my_bucket, bucket_size, 0))
    slots = jnp.arange(slot_cap, dtype=jnp.int32)
    valid = slots < row_size
    padding = jnp.zeros((slot_cap,), jnp.float32)
    sender = (lax.axis_index("ctx") == 0) & valid
    own_state = jnp.where(sender, jnp.stack([adam_mean[0], adam_square[0]]), 0.0)
    laid = lax.dynamic_update_slice(
        jnp.zeros((2, total_len + slot_cap), jnp.float32), own_state, (0, row_begin)
    )[:, :total_len]
    summed = tree_sum(tree_sum(jnp.concatenate([grad_part[None], laid]), "ctx"), "dp")
    gradient = summed[0]
    mean_flat = summed[1]
    square_flat = summed[2]
    grad_norm = jnp.sqrt(jnp.sum(gradient * gradient))
    shrink = jnp.minimum(1.0, clip_norm / (grad_norm + 1e-06))
    grad_row = (
        jnp.where(
            valid,
            lax.dynamic_slice_in_dim(jnp.concatenate([gradient, padding]), row_begin, slot_cap),
            0.0,
        )
        * shrink
    )
    new_mean = beta_one * adam_mean[0] + (1.0 - beta_one) * grad_row
    new_square = beta_two * adam_square[0] + (1.0 - beta_two) * grad_row * grad_row
    grad_flat = gradient * shrink
    mean_all = beta_one * mean_flat + (1.0 - beta_one) * grad_flat
    square_all = beta_two * square_flat + (1.0 - beta_two) * grad_flat * grad_flat
    direction = (
        mean_all
        / (1.0 - beta_one**step_count)
        / (jnp.sqrt(square_all / (1.0 - beta_two**step_count)) + adam_eps)
    )
    new_params = parameters - learn_rate * direction
    return (
        normed,
        grad_hidden,
        grad_gating,
        grad_dt,
        grad_b,
        grad_c,
        new_params,
        new_mean[None],
        new_square[None],
    )


def solution(mesh):
    return jax.shard_map(
        on_device,
        mesh=mesh,
        in_specs=(
            P("dp", "ctx", None),
            P("dp", "ctx", None),
            P("dp", "ctx", None),
            P("dp", "ctx", None),
            P("dp", "ctx", None),
            P("dp", None),
            P("dp", "ctx", None),
            P(),
            P("dp", None),
            P("dp", None),
            P(),
            P(),
        ),
        out_specs=(
            P("dp", "ctx", None),
            P("dp", "ctx", None),
            P("dp", "ctx", None),
            P("dp", "ctx", None),
            P("dp", "ctx", None),
            P("dp", "ctx", None),
            P(),
            P("dp", None),
            P("dp", None),
        ),
        check_vma=False,
    )
```

```python
import jax
import jax.numpy as jnp
from jax import lax
from jax.sharding import PartitionSpec as P

SPAN = 256
CH = 3072


eps_norm = 1e-05
clip_norm = 64.0
beta_one = 0.9
beta_two = 0.95
adam_eps = 1e-08
learn_rate = 0.02
step_count = 100.0
highest = lax.Precision.HIGHEST


def exchange(x):
    n = x.shape[0]
    idx = lax.axis_index("ctx")
    out = lax.dynamic_update_index_in_dim(
        jnp.zeros_like(x), lax.dynamic_index_in_dim(x, idx, 0), idx, 0
    )
    for k in range(1, n):
        send = lax.dynamic_index_in_dim(x, (idx + k) % n, 0)
        got = lax.ppermute(send, "ctx", [(i, (i + k) % n) for i in range(n)])
        out = lax.dynamic_update_index_in_dim(out, got, (idx + n - k) % n, 0)
    return out


def to_heads(x, groups):
    _, t, c = x.shape
    x = x.reshape(t, groups, c // groups).transpose(1, 0, 2)
    x = exchange(x)
    return x.reshape(groups * t, c // groups)


def from_heads(x, groups):
    tw, w = x.shape
    x = x.reshape(groups, tw // groups, w)
    return exchange(x)


def to_positions(x, groups):
    parts = from_heads(x, groups)
    _, t, w = parts.shape
    return parts.transpose(1, 0, 2).reshape(1, t, groups * w)


def tree_sum(x, axis):
    size = lax.axis_size(axis)
    if size & (size - 1):
        return lax.psum(x, axis)
    step = 1
    while step < size:
        x = x + lax.ppermute(x, axis, [(i, i ^ step) for i in range(size)])
        step *= 2
    return x


def rounded(value):
    return lax.optimization_barrier(value.astype(jnp.bfloat16)).astype(jnp.float32)


def ssd_group(hidden, dt_raw, b_input, c_input, resets, a_log, dt_bias, skip):
    length = hidden.shape[0]
    heads = a_log.shape[0]
    width = hidden.shape[1] // heads
    blocks = length // SPAN
    step_sizes = jax.nn.softplus(dt_raw.astype(jnp.float32) + dt_bias)
    log_decay = (step_sizes * -jnp.exp(a_log)).reshape(blocks, SPAN, heads).transpose(0, 2, 1)
    lower = (jnp.arange(SPAN)[:, None] >= jnp.arange(SPAN)[None, :]).astype(jnp.float32)
    cumul = jnp.einsum("chs,ts->cht", log_decay, lower, precision=highest)
    inputs = hidden.astype(jnp.float32).reshape(blocks, SPAN, heads, width)
    scaled = rounded(inputs * step_sizes.reshape(blocks, SPAN, heads, 1))
    b_rows = b_input.astype(jnp.float32).reshape(blocks, SPAN, -1)
    c_rows = c_input.astype(jnp.float32).reshape(blocks, SPAN, -1)
    scores = jnp.einsum("ctn,csn->cts", c_rows, b_rows, precision=highest)
    causal = jnp.arange(SPAN)[:, None] >= jnp.arange(SPAN)[None, :]
    spread = cumul[:, :, :, None] - cumul[:, :, None, :]
    decay = jnp.where(causal, jnp.exp(jnp.where(causal, spread, 0.0)), 0.0)
    weights = rounded(scores[:, None] * decay)
    intra = jnp.einsum("chts,cshp->cthp", weights, scaled, precision=highest)
    tail = cumul[:, :, -1:] - cumul
    b_decayed = rounded(b_rows[:, None] * jnp.exp(tail)[..., None])
    block_state = jnp.einsum("chsn,cshp->chnp", b_decayed, scaled, precision=highest)
    keep = 1.0 - resets.astype(jnp.float32)

    def advance(state, items):
        keep_one, total, added = items
        entering = state * keep_one
        return (jnp.exp(total)[:, None, None] * entering + added, entering)

    start_state = jnp.zeros(block_state.shape[1:], jnp.float32)
    last_state, entering = lax.scan(
        advance, start_state, (keep, cumul[:, :, -1], block_state), unroll=True
    )
    c_decayed = rounded(c_rows[:, None] * jnp.exp(cumul)[..., None])
    inter = jnp.einsum("chtn,chnp->cthp", c_decayed, rounded(entering), precision=highest)
    output = intra + inter + skip[:, None] * inputs
    return output.reshape(length, heads * width).astype(jnp.bfloat16)


def gate_values(y_values, gating):
    gated = y_values.astype(jnp.float32) * jax.nn.silu(gating.astype(jnp.float32))
    return (gated, jnp.sum(gated * gated, axis=-1))


def normalize(gated, total, gain):
    factor = lax.rsqrt(total / CH + eps_norm)
    return (factor, (gated * factor[..., None] * gain).astype(jnp.bfloat16))


def norm_backward(cotangent, gain, gated, factor, dot_total, y_values, gating):
    upstream = cotangent.astype(jnp.float32) * gain
    d_gated = (
        upstream * factor[..., None]
        - gated * (factor * factor * factor * dot_total / CH)[..., None]
    )
    gate_f = gating.astype(jnp.float32)
    sigma = jax.nn.sigmoid(gate_f)
    d_y = (d_gated * (gate_f * sigma)).astype(jnp.bfloat16)
    d_gate = (
        d_gated * y_values.astype(jnp.float32) * sigma * (1.0 + gate_f * (1.0 - sigma))
    ).astype(jnp.bfloat16)
    d_gain = jnp.sum(
        cotangent.astype(jnp.float32) * gated * factor[..., None], axis=tuple(range(gated.ndim - 1))
    )
    return (d_y, d_gate, d_gain)


def on_device(
    hidden,
    gating,
    dt_raw,
    b_input,
    c_input,
    resets,
    cotangent,
    parameters,
    adam_mean,
    adam_square,
    bucket_size,
    bucket_owner,
):
    heads_all = dt_raw.shape[2]
    groups = lax.axis_size("ctx")
    group = heads_all // groups
    state_size = b_input.shape[2]
    tokens = hidden.shape[1]
    first = lax.axis_index("ctx") * group
    head_params = parameters[: 3 * heads_all].reshape(3, heads_all)
    gain = parameters[3 * heads_all :]
    local_params = lax.dynamic_slice_in_dim(head_params, first, group, 1)
    width = hidden.shape[2] // groups
    shared = jnp.concatenate([b_input[0], c_input[0]], axis=1)
    packed = jnp.concatenate(
        [
            hidden[0].reshape(tokens, groups, width).transpose(1, 0, 2),
            jnp.broadcast_to(shared[None], (groups,) + shared.shape),
            dt_raw[0].reshape(tokens, groups, group).transpose(1, 0, 2),
        ],
        axis=2,
    )
    arrived = exchange(packed).reshape(groups * tokens, -1)
    b_all = arrived[None, :, width : width + state_size]
    c_all = arrived[None, :, width + state_size : width + 2 * state_size]
    seq_resets = resets[0]

    def local_fn(x_arg, dt_arg, b_arg, c_arg, a_arg, bias_arg, skip_arg):
        return ssd_group(x_arg, dt_arg, b_arg, c_arg, seq_resets, a_arg, bias_arg, skip_arg)

    x_heads = arrived[None, :, :width]
    dt_heads = arrived[None, :, width + 2 * state_size :]
    y_heads, pullback = jax.vjp(
        local_fn,
        x_heads[0],
        dt_heads[0],
        b_all[0],
        c_all[0],
        local_params[0],
        local_params[1],
        local_params[2],
    )
    y_seq = to_positions(y_heads, groups)
    gated, total = gate_values(y_seq, gating)
    factor, normed = normalize(gated, total, gain)
    dot_total = jnp.sum(cotangent.astype(jnp.float32) * gain * gated, axis=-1)
    d_y, grad_gating, d_gain = norm_backward(
        cotangent, gain, gated, factor, dot_total, y_seq, gating
    )
    d_y_heads = to_heads(d_y, groups)[None]
    d_x, d_dt, d_b, d_c, d_alog, d_bias, d_skip = pullback(d_y_heads[0])
    back = from_heads(jnp.concatenate([d_x, d_b, d_c, d_dt], axis=-1), groups)
    grad_hidden = back[..., :width].transpose(1, 0, 2).reshape(1, tokens, groups * width)
    grad_dt = back[..., width + 2 * state_size :].transpose(1, 0, 2).reshape(1, tokens, heads_all)
    pair_sum = jnp.sum(
        back[..., width : width + 2 * state_size].astype(jnp.float32), axis=0
    )[None].astype(jnp.bfloat16)
    grad_b = pair_sum[..., :state_size]
    grad_c = pair_sum[..., state_size:]
    head_grads = jnp.stack([d_alog, d_bias, d_skip])
    full_heads = lax.dynamic_update_slice(
        jnp.zeros((3, heads_all), jnp.float32), head_grads, (0, first)
    )
    grad_part = jnp.concatenate([full_heads.reshape(-1), d_gain])
    owners = lax.axis_size("dp")
    slot_cap = adam_mean.shape[1]
    total_len = parameters.shape[0]
    ends = jnp.cumsum(bucket_size)
    begins = ends - bucket_size
    order = jnp.arange(owners, dtype=jnp.int32)
    mine = lax.axis_index("dp")
    my_bucket = jnp.sum(jnp.where(bucket_owner == mine, order, 0))
    row_begin = jnp.sum(jnp.where(order == my_bucket, begins, 0))
    row_size = jnp.sum(jnp.where(order == my_bucket, bucket_size, 0))
    slots = jnp.arange(slot_cap, dtype=jnp.int32)
    valid = slots < row_size
    padding = jnp.zeros((slot_cap,), jnp.float32)
    sender = (lax.axis_index("ctx") == 0) & valid
    own_state = jnp.where(sender, jnp.stack([adam_mean[0], adam_square[0]]), 0.0)
    laid = lax.dynamic_update_slice(
        jnp.zeros((2, total_len + slot_cap), jnp.float32), own_state, (0, row_begin)
    )[:, :total_len]
    summed = tree_sum(tree_sum(jnp.concatenate([grad_part[None], laid]), "ctx"), "dp")
    gradient = summed[0]
    mean_flat = summed[1]
    square_flat = summed[2]
    grad_norm = jnp.sqrt(jnp.sum(gradient * gradient))
    shrink = jnp.minimum(1.0, clip_norm / (grad_norm + 1e-06))
    grad_row = (
        jnp.where(
            valid,
            lax.dynamic_slice_in_dim(jnp.concatenate([gradient, padding]), row_begin, slot_cap),
            0.0,
        )
        * shrink
    )
    new_mean = beta_one * adam_mean[0] + (1.0 - beta_one) * grad_row
    new_square = beta_two * adam_square[0] + (1.0 - beta_two) * grad_row * grad_row
    grad_flat = gradient * shrink
    mean_all = beta_one * mean_flat + (1.0 - beta_one) * grad_flat
    square_all = beta_two * square_flat + (1.0 - beta_two) * grad_flat * grad_flat
    direction = (
        mean_all
        / (1.0 - beta_one**step_count)
        / (jnp.sqrt(square_all / (1.0 - beta_two**step_count)) + adam_eps)
    )
    new_params = parameters - learn_rate * direction
    return (
        normed,
        grad_hidden,
        grad_gating,
        grad_dt,
        grad_b,
        grad_c,
        new_params,
        new_mean[None],
        new_square[None],
    )


def solution(mesh):
    return jax.shard_map(
        on_device,
        mesh=mesh,
        in_specs=(
            P("dp", "ctx", None),
            P("dp", "ctx", None),
            P("dp", "ctx", None),
            P("dp", "ctx", None),
            P("dp", "ctx", None),
            P("dp", None),
            P("dp", "ctx", None),
            P(),
            P("dp", None),
            P("dp", None),
            P(),
            P(),
        ),
        out_specs=(
            P("dp", "ctx", None),
            P("dp", "ctx", None),
            P("dp", "ctx", None),
            P("dp", "ctx", None),
            P("dp", "ctx", None),
            P("dp", "ctx", None),
            P(),
            P("dp", None),
            P("dp", None),
        ),
        check_vma=False,
    )
```

```python
import jax
import jax.numpy as jnp
from jax import lax
from jax.sharding import PartitionSpec as P

SPAN = 256
CH = 3072


eps_norm = 1e-05
clip_norm = 64.0
beta_one = 0.9
beta_two = 0.95
adam_eps = 1e-08
learn_rate = 0.02
step_count = 100.0
highest = lax.Precision.HIGHEST


def to_heads(x, groups):
    _, t, c = x.shape
    x = x.reshape(t, groups, c // groups).transpose(1, 0, 2)
    x = lax.all_to_all(x, "ctx", 0, 0, tiled=True)
    return x.reshape(groups * t, c // groups)


def from_heads(x, groups):
    tw, w = x.shape
    x = x.reshape(groups, tw // groups, w)
    return lax.all_to_all(x, "ctx", 0, 0, tiled=True)


def to_positions(x, groups):
    parts = from_heads(x, groups)
    _, t, w = parts.shape
    return parts.transpose(1, 0, 2).reshape(1, t, groups * w)


def tree_sum(x, axis):
    size = lax.axis_size(axis)
    if size & (size - 1):
        return lax.psum(x, axis)
    step = 1
    while step < size:
        x = x + lax.ppermute(x, axis, [(i, i ^ step) for i in range(size)])
        step *= 2
    return x


def rounded(value):
    return lax.optimization_barrier(value.astype(jnp.bfloat16)).astype(jnp.float32)


def ssd_group(hidden, dt_raw, b_input, c_input, resets, a_log, dt_bias, skip):
    length = hidden.shape[0]
    heads = a_log.shape[0]
    width = hidden.shape[1] // heads
    blocks = length // SPAN
    step_sizes = jax.nn.softplus(dt_raw.astype(jnp.float32) + dt_bias)
    log_decay = (step_sizes * -jnp.exp(a_log)).reshape(blocks, SPAN, heads).transpose(0, 2, 1)
    lower = (jnp.arange(SPAN)[:, None] >= jnp.arange(SPAN)[None, :]).astype(jnp.float32)
    cumul = jnp.einsum("chs,ts->cht", log_decay, lower, precision=highest)
    inputs = hidden.astype(jnp.float32).reshape(blocks, SPAN, heads, width)
    scaled = rounded(inputs * step_sizes.reshape(blocks, SPAN, heads, 1))
    b_rows = b_input.astype(jnp.float32).reshape(blocks, SPAN, -1)
    c_rows = c_input.astype(jnp.float32).reshape(blocks, SPAN, -1)
    scores = jnp.einsum("ctn,csn->cts", c_rows, b_rows, precision=highest)
    causal = jnp.arange(SPAN)[:, None] >= jnp.arange(SPAN)[None, :]
    spread = cumul[:, :, :, None] - cumul[:, :, None, :]
    decay = jnp.where(causal, jnp.exp(jnp.where(causal, spread, 0.0)), 0.0)
    weights = rounded(scores[:, None] * decay)
    intra = jnp.einsum("chts,cshp->cthp", weights, scaled, precision=highest)
    tail = cumul[:, :, -1:] - cumul
    b_decayed = rounded(b_rows[:, None] * jnp.exp(tail)[..., None])
    block_state = jnp.einsum("chsn,cshp->chnp", b_decayed, scaled, precision=highest)
    keep = 1.0 - resets.astype(jnp.float32)

    def advance(state, items):
        keep_one, total, added = items
        entering = state * keep_one
        return (jnp.exp(total)[:, None, None] * entering + added, entering)

    start_state = jnp.zeros(block_state.shape[1:], jnp.float32)
    _, entering = lax.scan(advance, start_state, (keep, cumul[:, :, -1], block_state), unroll=True)
    c_decayed = rounded(c_rows[:, None] * jnp.exp(cumul)[..., None])
    inter = jnp.einsum("chtn,chnp->cthp", c_decayed, rounded(entering), precision=highest)
    output = intra + inter + skip[:, None] * inputs
    return output.reshape(length, heads * width).astype(jnp.bfloat16)


def gate_values(y_values, gating):
    gated = y_values.astype(jnp.float32) * jax.nn.silu(gating.astype(jnp.float32))
    return (gated, jnp.sum(gated * gated, axis=-1))


def normalize(gated, total, gain):
    factor = lax.rsqrt(total / CH + eps_norm)
    return (factor, (gated * factor[..., None] * gain).astype(jnp.bfloat16))


def norm_backward(cotangent, gain, gated, factor, dot_total, y_values, gating):
    upstream = cotangent.astype(jnp.float32) * gain
    d_gated = (
        upstream * factor[..., None]
        - gated * (factor * factor * factor * dot_total / CH)[..., None]
    )
    gate_f = gating.astype(jnp.float32)
    sigma = jax.nn.sigmoid(gate_f)
    d_y = (d_gated * (gate_f * sigma)).astype(jnp.bfloat16)
    d_gate = (
        d_gated * y_values.astype(jnp.float32) * sigma * (1.0 + gate_f * (1.0 - sigma))
    ).astype(jnp.bfloat16)
    d_gain = jnp.sum(
        cotangent.astype(jnp.float32) * gated * factor[..., None], axis=tuple(range(gated.ndim - 1))
    )
    return (d_y, d_gate, d_gain)


def on_device(
    hidden,
    gating,
    dt_raw,
    b_input,
    c_input,
    resets,
    cotangent,
    parameters,
    adam_mean,
    adam_square,
    bucket_size,
    bucket_owner,
):
    heads_all = dt_raw.shape[2]
    groups = lax.axis_size("ctx")
    group = heads_all // groups
    state_size = b_input.shape[2]
    tokens = hidden.shape[1]
    first = lax.axis_index("ctx") * group
    head_params = parameters[: 3 * heads_all].reshape(3, heads_all)
    gain = parameters[3 * heads_all :]
    local_params = lax.dynamic_slice_in_dim(head_params, first, group, 1)
    width = hidden.shape[2] // groups
    shared = jnp.concatenate([b_input[0], c_input[0]], axis=1)
    packed = jnp.concatenate(
        [
            hidden[0].reshape(tokens, groups, width).transpose(1, 0, 2),
            jnp.broadcast_to(shared[None], (groups,) + shared.shape),
            dt_raw[0].reshape(tokens, groups, group).transpose(1, 0, 2),
        ],
        axis=2,
    )
    arrived = lax.all_to_all(packed, "ctx", 0, 0, tiled=True).reshape(groups * tokens, -1)
    b_all = arrived[None, :, width : width + state_size]
    c_all = arrived[None, :, width + state_size : width + 2 * state_size]
    seq_resets = resets[0]

    def local_fn(x_arg, dt_arg, b_arg, c_arg, a_arg, bias_arg, skip_arg):
        return ssd_group(x_arg, dt_arg, b_arg, c_arg, seq_resets, a_arg, bias_arg, skip_arg)

    x_heads = arrived[None, :, :width]
    dt_heads = arrived[None, :, width + 2 * state_size :]
    y_heads, pullback = jax.vjp(
        local_fn,
        x_heads[0],
        dt_heads[0],
        b_all[0],
        c_all[0],
        local_params[0],
        local_params[1],
        local_params[2],
    )
    y_seq = to_positions(y_heads, groups)
    gated, total = gate_values(y_seq, gating)
    factor, normed = normalize(gated, total, gain)
    dot_total = jnp.sum(cotangent.astype(jnp.float32) * gain * gated, axis=-1)
    d_y, grad_gating, d_gain = norm_backward(
        cotangent, gain, gated, factor, dot_total, y_seq, gating
    )
    d_y_heads = to_heads(d_y, groups)[None]
    d_x, d_dt, d_b, d_c, d_alog, d_bias, d_skip = pullback(d_y_heads[0])
    back = from_heads(jnp.concatenate([d_x, d_b, d_c, d_dt], axis=-1), groups)
    grad_hidden = back[..., :width].transpose(1, 0, 2).reshape(1, tokens, groups * width)
    grad_dt = back[..., width + 2 * state_size :].transpose(1, 0, 2).reshape(1, tokens, heads_all)
    pair_sum = jnp.sum(
        back[..., width : width + 2 * state_size].astype(jnp.float32), axis=0
    )[None].astype(jnp.bfloat16)
    grad_b = pair_sum[..., :state_size]
    grad_c = pair_sum[..., state_size:]
    head_grads = jnp.stack([d_alog, d_bias, d_skip])
    full_heads = lax.dynamic_update_slice(
        jnp.zeros((3, heads_all), jnp.float32), head_grads, (0, first)
    )
    grad_part = jnp.concatenate([full_heads.reshape(-1), d_gain])
    owners = lax.axis_size("dp")
    slot_cap = adam_mean.shape[1]
    total_len = parameters.shape[0]
    ends = jnp.cumsum(bucket_size)
    begins = ends - bucket_size
    order = jnp.arange(owners, dtype=jnp.int32)
    mine = lax.axis_index("dp")
    my_bucket = jnp.sum(jnp.where(bucket_owner == mine, order, 0))
    row_begin = jnp.sum(jnp.where(order == my_bucket, begins, 0))
    row_size = jnp.sum(jnp.where(order == my_bucket, bucket_size, 0))
    slots = jnp.arange(slot_cap, dtype=jnp.int32)
    valid = slots < row_size
    padding = jnp.zeros((slot_cap,), jnp.float32)
    sender = (lax.axis_index("ctx") == 0) & valid
    own_state = jnp.where(sender, jnp.stack([adam_mean[0], adam_square[0]]), 0.0)
    laid = lax.dynamic_update_slice(
        jnp.zeros((2, total_len + slot_cap), jnp.float32), own_state, (0, row_begin)
    )[:, :total_len]
    summed = tree_sum(tree_sum(jnp.concatenate([grad_part[None], laid]), "dp"), "ctx")
    gradient = summed[0]
    mean_flat = summed[1]
    square_flat = summed[2]
    grad_norm = jnp.sqrt(jnp.sum(gradient * gradient))
    shrink = jnp.minimum(1.0, clip_norm / (grad_norm + 1e-06))
    grad_row = (
        jnp.where(
            valid,
            lax.dynamic_slice_in_dim(jnp.concatenate([gradient, padding]), row_begin, slot_cap),
            0.0,
        )
        * shrink
    )
    new_mean = beta_one * adam_mean[0] + (1.0 - beta_one) * grad_row
    new_square = beta_two * adam_square[0] + (1.0 - beta_two) * grad_row * grad_row
    grad_flat = gradient * shrink
    mean_all = beta_one * mean_flat + (1.0 - beta_one) * grad_flat
    square_all = beta_two * square_flat + (1.0 - beta_two) * grad_flat * grad_flat
    direction = (
        mean_all
        / (1.0 - beta_one**step_count)
        / (jnp.sqrt(square_all / (1.0 - beta_two**step_count)) + adam_eps)
    )
    new_params = parameters - learn_rate * direction
    return (
        normed,
        grad_hidden,
        grad_gating,
        grad_dt,
        grad_b,
        grad_c,
        new_params,
        new_mean[None],
        new_square[None],
    )


def solution(mesh):
    return jax.shard_map(
        on_device,
        mesh=mesh,
        in_specs=(
            P("dp", "ctx", None),
            P("dp", "ctx", None),
            P("dp", "ctx", None),
            P("dp", "ctx", None),
            P("dp", "ctx", None),
            P("dp", None),
            P("dp", "ctx", None),
            P(),
            P("dp", None),
            P("dp", None),
            P(),
            P(),
        ),
        out_specs=(
            P("dp", "ctx", None),
            P("dp", "ctx", None),
            P("dp", "ctx", None),
            P("dp", "ctx", None),
            P("dp", "ctx", None),
            P("dp", "ctx", None),
            P(),
            P("dp", None),
            P("dp", None),
        ),
        check_vma=False,
    )
```

```python
import jax
import jax.numpy as jnp
from jax import lax
from jax.sharding import PartitionSpec as P

SPAN = 256
CH = 3072


eps_norm = 1e-05
clip_norm = 64.0
beta_one = 0.9
beta_two = 0.95
adam_eps = 1e-08
learn_rate = 0.02
step_count = 100.0
highest = lax.Precision.HIGHEST


def to_heads(x, groups):
    _, t, c = x.shape
    x = x.reshape(t, groups, c // groups).transpose(1, 0, 2)
    x = lax.all_to_all(x, "ctx", 0, 0, tiled=True)
    return x.reshape(groups * t, c // groups)


def from_heads(x, groups):
    tw, w = x.shape
    x = x.reshape(groups, tw // groups, w)
    return lax.all_to_all(x, "ctx", 0, 0, tiled=True)


def to_positions(x, groups):
    parts = from_heads(x, groups)
    _, t, w = parts.shape
    return parts.transpose(1, 0, 2).reshape(1, t, groups * w)


def tree_sum(x, axis):
    size = lax.axis_size(axis)
    if size & (size - 1):
        return lax.psum(x, axis)
    idx = lax.axis_index(axis)
    step = 1
    while step * 4 <= size:
        got = [x] + [
            lax.ppermute(x, axis, [(i, i ^ (k * step)) for i in range(size)]) for k in (1, 2, 3)
        ]
        held = jnp.stack(got)
        place = (idx // step) % 4
        parts = [lax.dynamic_index_in_dim(held, place ^ m, 0, keepdims=False) for m in range(4)]
        x = (parts[0] + parts[1]) + (parts[2] + parts[3])
        step *= 4
    while step < size:
        x = x + lax.ppermute(x, axis, [(i, i ^ step) for i in range(size)])
        step *= 2
    return x


def rounded(value):
    return lax.optimization_barrier(value.astype(jnp.bfloat16)).astype(jnp.float32)


def ssd_group(hidden, dt_raw, b_input, c_input, resets, a_log, dt_bias, skip):
    length = hidden.shape[0]
    heads = a_log.shape[0]
    width = hidden.shape[1] // heads
    blocks = length // SPAN
    step_sizes = jax.nn.softplus(dt_raw.astype(jnp.float32) + dt_bias)
    log_decay = (step_sizes * -jnp.exp(a_log)).reshape(blocks, SPAN, heads).transpose(0, 2, 1)
    lower = (jnp.arange(SPAN)[:, None] >= jnp.arange(SPAN)[None, :]).astype(jnp.float32)
    cumul = jnp.einsum("chs,ts->cht", log_decay, lower, precision=highest)
    inputs = hidden.astype(jnp.float32).reshape(blocks, SPAN, heads, width)
    scaled = rounded(inputs * step_sizes.reshape(blocks, SPAN, heads, 1))
    b_rows = b_input.astype(jnp.float32).reshape(blocks, SPAN, -1)
    c_rows = c_input.astype(jnp.float32).reshape(blocks, SPAN, -1)
    scores = jnp.einsum("ctn,csn->cts", c_rows, b_rows, precision=highest)
    causal = jnp.arange(SPAN)[:, None] >= jnp.arange(SPAN)[None, :]
    spread = cumul[:, :, :, None] - cumul[:, :, None, :]
    decay = jnp.where(causal, jnp.exp(jnp.where(causal, spread, 0.0)), 0.0)
    weights = rounded(scores[:, None] * decay)
    intra = jnp.einsum("chts,cshp->cthp", weights, scaled, precision=highest)
    tail = cumul[:, :, -1:] - cumul
    b_decayed = rounded(b_rows[:, None] * jnp.exp(tail)[..., None])
    block_state = jnp.einsum("chsn,cshp->chnp", b_decayed, scaled, precision=highest)
    keep = 1.0 - resets.astype(jnp.float32)

    def advance(state, items):
        keep_one, total, added = items
        entering = state * keep_one
        return (jnp.exp(total)[:, None, None] * entering + added, entering)

    start_state = jnp.zeros(block_state.shape[1:], jnp.float32)
    _, entering = lax.scan(advance, start_state, (keep, cumul[:, :, -1], block_state), unroll=True)
    c_decayed = rounded(c_rows[:, None] * jnp.exp(cumul)[..., None])
    inter = jnp.einsum("chtn,chnp->cthp", c_decayed, rounded(entering), precision=highest)
    output = intra + inter + skip[:, None] * inputs
    return output.reshape(length, heads * width).astype(jnp.bfloat16)


def gate_values(y_values, gating):
    gated = y_values.astype(jnp.float32) * jax.nn.silu(gating.astype(jnp.float32))
    return (gated, jnp.sum(gated * gated, axis=-1))


def normalize(gated, total, gain):
    factor = lax.rsqrt(total / CH + eps_norm)
    return (factor, (gated * factor[..., None] * gain).astype(jnp.bfloat16))


def norm_backward(cotangent, gain, gated, factor, dot_total, y_values, gating):
    upstream = cotangent.astype(jnp.float32) * gain
    d_gated = (
        upstream * factor[..., None]
        - gated * (factor * factor * factor * dot_total / CH)[..., None]
    )
    gate_f = gating.astype(jnp.float32)
    sigma = jax.nn.sigmoid(gate_f)
    d_y = (d_gated * (gate_f * sigma)).astype(jnp.bfloat16)
    d_gate = (
        d_gated * y_values.astype(jnp.float32) * sigma * (1.0 + gate_f * (1.0 - sigma))
    ).astype(jnp.bfloat16)
    d_gain = jnp.sum(
        cotangent.astype(jnp.float32) * gated * factor[..., None], axis=tuple(range(gated.ndim - 1))
    )
    return (d_y, d_gate, d_gain)


def on_device(
    hidden,
    gating,
    dt_raw,
    b_input,
    c_input,
    resets,
    cotangent,
    parameters,
    adam_mean,
    adam_square,
    bucket_size,
    bucket_owner,
):
    heads_all = dt_raw.shape[2]
    groups = lax.axis_size("ctx")
    group = heads_all // groups
    state_size = b_input.shape[2]
    tokens = hidden.shape[1]
    first = lax.axis_index("ctx") * group
    head_params = parameters[: 3 * heads_all].reshape(3, heads_all)
    gain = parameters[3 * heads_all :]
    local_params = lax.dynamic_slice_in_dim(head_params, first, group, 1)
    width = hidden.shape[2] // groups
    shared = jnp.concatenate([b_input[0], c_input[0]], axis=1)
    small = jnp.concatenate(
        [
            jnp.broadcast_to(shared[None], (groups,) + shared.shape),
            dt_raw[0].reshape(tokens, groups, group).transpose(1, 0, 2),
        ],
        axis=2,
    )
    small_in = lax.all_to_all(small, "ctx", 0, 0, tiled=True).reshape(groups * tokens, -1)
    x_in = to_heads(hidden, groups)
    b_all = small_in[None, :, :state_size]
    c_all = small_in[None, :, state_size : 2 * state_size]
    seq_resets = resets[0]

    def local_fn(x_arg, dt_arg, b_arg, c_arg, a_arg, bias_arg, skip_arg):
        return ssd_group(x_arg, dt_arg, b_arg, c_arg, seq_resets, a_arg, bias_arg, skip_arg)

    x_heads = x_in[None]
    dt_heads = small_in[None, :, 2 * state_size :]
    y_heads, pullback = jax.vjp(
        local_fn,
        x_heads[0],
        dt_heads[0],
        b_all[0],
        c_all[0],
        local_params[0],
        local_params[1],
        local_params[2],
    )
    y_seq = to_positions(y_heads, groups)
    gated, total = gate_values(y_seq, gating)
    factor, normed = normalize(gated, total, gain)
    dot_total = jnp.sum(cotangent.astype(jnp.float32) * gain * gated, axis=-1)
    d_y, grad_gating, d_gain = norm_backward(
        cotangent, gain, gated, factor, dot_total, y_seq, gating
    )
    d_y_heads = to_heads(d_y, groups)[None]
    d_x, d_dt, d_b, d_c, d_alog, d_bias, d_skip = pullback(d_y_heads[0])
    back = from_heads(jnp.concatenate([d_x, d_b, d_c, d_dt], axis=-1), groups)
    grad_hidden = back[..., :width].transpose(1, 0, 2).reshape(1, tokens, groups * width)
    grad_dt = back[..., width + 2 * state_size :].transpose(1, 0, 2).reshape(1, tokens, heads_all)
    pair_sum = jnp.sum(
        back[..., width : width + 2 * state_size].astype(jnp.float32), axis=0
    )[None].astype(jnp.bfloat16)
    grad_b = pair_sum[..., :state_size]
    grad_c = pair_sum[..., state_size:]
    head_grads = jnp.stack([d_alog, d_bias, d_skip])
    full_heads = lax.dynamic_update_slice(
        jnp.zeros((3, heads_all), jnp.float32), head_grads, (0, first)
    )
    grad_part = jnp.concatenate([full_heads.reshape(-1), d_gain])
    owners = lax.axis_size("dp")
    slot_cap = adam_mean.shape[1]
    total_len = parameters.shape[0]
    ends = jnp.cumsum(bucket_size)
    begins = ends - bucket_size
    order = jnp.arange(owners, dtype=jnp.int32)
    mine = lax.axis_index("dp")
    my_bucket = jnp.sum(jnp.where(bucket_owner == mine, order, 0))
    row_begin = jnp.sum(jnp.where(order == my_bucket, begins, 0))
    row_size = jnp.sum(jnp.where(order == my_bucket, bucket_size, 0))
    slots = jnp.arange(slot_cap, dtype=jnp.int32)
    valid = slots < row_size
    padding = jnp.zeros((slot_cap,), jnp.float32)
    sender = (lax.axis_index("ctx") == 0) & valid
    own_state = jnp.where(sender, jnp.stack([adam_mean[0], adam_square[0]]), 0.0)
    laid = lax.dynamic_update_slice(
        jnp.zeros((2, total_len + slot_cap), jnp.float32), own_state, (0, row_begin)
    )[:, :total_len]
    summed = tree_sum(tree_sum(jnp.concatenate([grad_part[None], laid]), "dp"), "ctx")
    gradient = summed[0]
    mean_flat = summed[1]
    square_flat = summed[2]
    grad_norm = jnp.sqrt(jnp.sum(gradient * gradient))
    shrink = jnp.minimum(1.0, clip_norm / (grad_norm + 1e-06))
    grad_row = (
        jnp.where(
            valid,
            lax.dynamic_slice_in_dim(jnp.concatenate([gradient, padding]), row_begin, slot_cap),
            0.0,
        )
        * shrink
    )
    new_mean = beta_one * adam_mean[0] + (1.0 - beta_one) * grad_row
    new_square = beta_two * adam_square[0] + (1.0 - beta_two) * grad_row * grad_row
    grad_flat = gradient * shrink
    mean_all = beta_one * mean_flat + (1.0 - beta_one) * grad_flat
    square_all = beta_two * square_flat + (1.0 - beta_two) * grad_flat * grad_flat
    direction = (
        mean_all
        / (1.0 - beta_one**step_count)
        / (jnp.sqrt(square_all / (1.0 - beta_two**step_count)) + adam_eps)
    )
    new_params = parameters - learn_rate * direction
    return (
        normed,
        grad_hidden,
        grad_gating,
        grad_dt,
        grad_b,
        grad_c,
        new_params,
        new_mean[None],
        new_square[None],
    )


def solution(mesh):
    return jax.shard_map(
        on_device,
        mesh=mesh,
        in_specs=(
            P("dp", "ctx", None),
            P("dp", "ctx", None),
            P("dp", "ctx", None),
            P("dp", "ctx", None),
            P("dp", "ctx", None),
            P("dp", None),
            P("dp", "ctx", None),
            P(),
            P("dp", None),
            P("dp", None),
            P(),
            P(),
        ),
        out_specs=(
            P("dp", "ctx", None),
            P("dp", "ctx", None),
            P("dp", "ctx", None),
            P("dp", "ctx", None),
            P("dp", "ctx", None),
            P("dp", "ctx", None),
            P(),
            P("dp", None),
            P("dp", None),
        ),
        check_vma=False,
    )
```

```python
import jax
import jax.numpy as jnp
from jax import lax
from jax.sharding import PartitionSpec as P

SPAN = 256
CH = 3072


eps_norm = 1e-05
clip_norm = 64.0
beta_one = 0.9
beta_two = 0.95
adam_eps = 1e-08
learn_rate = 0.02
step_count = 100.0
highest = lax.Precision.HIGHEST


def to_heads(x, groups):
    _, t, c = x.shape
    x = x.reshape(t, groups, c // groups).transpose(1, 0, 2)
    x = lax.all_to_all(x, "ctx", 0, 0, tiled=True)
    return x.reshape(groups * t, c // groups)


def from_heads(x, groups):
    tw, w = x.shape
    x = x.reshape(groups, tw // groups, w)
    return lax.all_to_all(x, "ctx", 0, 0, tiled=True)


def to_positions(x, groups):
    parts = from_heads(x, groups)
    _, t, w = parts.shape
    return parts.transpose(1, 0, 2).reshape(1, t, groups * w)


def tree_sum(x, axis):
    size = lax.axis_size(axis)
    if size & (size - 1):
        return lax.psum(x, axis)
    step = 1
    while step < size:
        x = x + lax.ppermute(x, axis, [(i, i ^ step) for i in range(size)])
        step *= 2
    return x


def rounded(value):
    return lax.optimization_barrier(value.astype(jnp.bfloat16)).astype(jnp.float32)


def ssd_group(hidden, dt_raw, b_input, c_input, resets, a_log, dt_bias, skip):
    length = hidden.shape[0]
    heads = a_log.shape[0]
    width = hidden.shape[1] // heads
    blocks = length // SPAN
    step_sizes = jax.nn.softplus(dt_raw.astype(jnp.float32) + dt_bias)
    log_decay = (step_sizes * -jnp.exp(a_log)).reshape(blocks, SPAN, heads).transpose(0, 2, 1)
    lower = (jnp.arange(SPAN)[:, None] >= jnp.arange(SPAN)[None, :]).astype(jnp.float32)
    cumul = jnp.einsum("chs,ts->cht", log_decay, lower, precision=highest)
    inputs = hidden.astype(jnp.float32).reshape(blocks, SPAN, heads, width)
    scaled = rounded(inputs * step_sizes.reshape(blocks, SPAN, heads, 1))
    b_rows = b_input.astype(jnp.float32).reshape(blocks, SPAN, -1)
    c_rows = c_input.astype(jnp.float32).reshape(blocks, SPAN, -1)
    scores = jnp.einsum("ctn,csn->cts", c_rows, b_rows, precision=highest)
    causal = jnp.arange(SPAN)[:, None] >= jnp.arange(SPAN)[None, :]
    spread = cumul[:, :, :, None] - cumul[:, :, None, :]
    decay = jnp.where(causal, jnp.exp(jnp.where(causal, spread, 0.0)), 0.0)
    weights = rounded(scores[:, None] * decay)
    intra = jnp.einsum("chts,cshp->cthp", weights, scaled, precision=highest)
    tail = cumul[:, :, -1:] - cumul
    b_decayed = rounded(b_rows[:, None] * jnp.exp(tail)[..., None])
    block_state = jnp.einsum("chsn,cshp->chnp", b_decayed, scaled, precision=highest)
    keep = 1.0 - resets.astype(jnp.float32)

    def advance(state, items):
        keep_one, total, added = items
        entering = state * keep_one
        return (jnp.exp(total)[:, None, None] * entering + added, entering)

    start_state = jnp.zeros(block_state.shape[1:], jnp.float32)
    _, entering = lax.scan(advance, start_state, (keep, cumul[:, :, -1], block_state), unroll=True)
    c_decayed = rounded(c_rows[:, None] * jnp.exp(cumul)[..., None])
    inter = jnp.einsum("chtn,chnp->cthp", c_decayed, rounded(entering), precision=highest)
    output = intra + inter + skip[:, None] * inputs
    return output.reshape(length, heads * width).astype(jnp.bfloat16)


def gate_values(y_values, gating):
    gated = y_values.astype(jnp.float32) * jax.nn.silu(gating.astype(jnp.float32))
    return (gated, jnp.sum(gated * gated, axis=-1))


def normalize(gated, total, gain):
    factor = lax.rsqrt(total / CH + eps_norm)
    return (factor, (gated * factor[..., None] * gain).astype(jnp.bfloat16))


def norm_backward(cotangent, gain, gated, factor, dot_total, y_values, gating):
    upstream = cotangent.astype(jnp.float32) * gain
    d_gated = (
        upstream * factor[..., None]
        - gated * (factor * factor * factor * dot_total / CH)[..., None]
    )
    gate_f = gating.astype(jnp.float32)
    sigma = jax.nn.sigmoid(gate_f)
    d_y = (d_gated * (gate_f * sigma)).astype(jnp.bfloat16)
    d_gate = (
        d_gated * y_values.astype(jnp.float32) * sigma * (1.0 + gate_f * (1.0 - sigma))
    ).astype(jnp.bfloat16)
    d_gain = jnp.sum(
        cotangent.astype(jnp.float32) * gated * factor[..., None], axis=tuple(range(gated.ndim - 1))
    )
    return (d_y, d_gate, d_gain)


def on_device(
    hidden,
    gating,
    dt_raw,
    b_input,
    c_input,
    resets,
    cotangent,
    parameters,
    adam_mean,
    adam_square,
    bucket_size,
    bucket_owner,
):
    heads_all = dt_raw.shape[2]
    groups = lax.axis_size("ctx")
    group = heads_all // groups
    state_size = b_input.shape[2]
    tokens = hidden.shape[1]
    first = lax.axis_index("ctx") * group
    head_params = parameters[: 3 * heads_all].reshape(3, heads_all)
    gain = parameters[3 * heads_all :]
    local_params = lax.dynamic_slice_in_dim(head_params, first, group, 1)
    width = hidden.shape[2] // groups
    shared = jnp.concatenate([b_input[0], c_input[0]], axis=1)
    small = jnp.concatenate(
        [
            jnp.broadcast_to(shared[None], (groups,) + shared.shape),
            dt_raw[0].reshape(tokens, groups, group).transpose(1, 0, 2),
        ],
        axis=2,
    )
    small_in = lax.all_to_all(small, "ctx", 0, 0, tiled=True).reshape(groups * tokens, -1)
    x_in = to_heads(hidden, groups)
    b_all = small_in[None, :, :state_size]
    c_all = small_in[None, :, state_size : 2 * state_size]
    seq_resets = resets[0]

    def local_fn(x_arg, dt_arg, b_arg, c_arg, a_arg, bias_arg, skip_arg):
        return ssd_group(x_arg, dt_arg, b_arg, c_arg, seq_resets, a_arg, bias_arg, skip_arg)

    x_heads = x_in[None]
    dt_heads = small_in[None, :, 2 * state_size :]
    y_heads, pullback = jax.vjp(
        local_fn,
        x_heads[0],
        dt_heads[0],
        b_all[0],
        c_all[0],
        local_params[0],
        local_params[1],
        local_params[2],
    )
    y_seq = to_positions(y_heads, groups)
    gated, total = gate_values(y_seq, gating)
    factor, normed = normalize(gated, total, gain)
    dot_total = jnp.sum(cotangent.astype(jnp.float32) * gain * gated, axis=-1)
    d_y, grad_gating, d_gain = norm_backward(
        cotangent, gain, gated, factor, dot_total, y_seq, gating
    )
    d_y_heads = to_heads(d_y, groups)[None]
    d_x, d_dt, d_b, d_c, d_alog, d_bias, d_skip = pullback(d_y_heads[0])
    back = from_heads(jnp.concatenate([d_x, d_b, d_c, d_dt], axis=-1), groups)
    grad_hidden = back[..., :width].transpose(1, 0, 2).reshape(1, tokens, groups * width)
    grad_dt = back[..., width + 2 * state_size :].transpose(1, 0, 2).reshape(1, tokens, heads_all)
    pair_sum = jnp.sum(
        back[..., width : width + 2 * state_size].astype(jnp.float32), axis=0
    )[None].astype(jnp.bfloat16)
    grad_b = pair_sum[..., :state_size]
    grad_c = pair_sum[..., state_size:]
    head_grads = jnp.stack([d_alog, d_bias, d_skip])
    full_heads = lax.dynamic_update_slice(
        jnp.zeros((3, heads_all), jnp.float32), head_grads, (0, first)
    )
    grad_part = jnp.concatenate([full_heads.reshape(-1), d_gain])
    owners = lax.axis_size("dp")
    slot_cap = adam_mean.shape[1]
    total_len = parameters.shape[0]
    ends = jnp.cumsum(bucket_size)
    begins = ends - bucket_size
    order = jnp.arange(owners, dtype=jnp.int32)
    mine = lax.axis_index("dp")
    my_bucket = jnp.sum(jnp.where(bucket_owner == mine, order, 0))
    row_begin = jnp.sum(jnp.where(order == my_bucket, begins, 0))
    row_size = jnp.sum(jnp.where(order == my_bucket, bucket_size, 0))
    slots = jnp.arange(slot_cap, dtype=jnp.int32)
    valid = slots < row_size
    padding = jnp.zeros((slot_cap,), jnp.float32)
    sender = (lax.axis_index("ctx") == 0) & valid
    own_state = jnp.where(sender, jnp.stack([adam_mean[0], adam_square[0]]), 0.0)
    laid = lax.dynamic_update_slice(
        jnp.zeros((2, total_len + slot_cap), jnp.float32), own_state, (0, row_begin)
    )[:, :total_len]
    summed = tree_sum(tree_sum(jnp.concatenate([grad_part[None], laid]), "dp"), "ctx")
    gradient = summed[0]
    mean_flat = summed[1]
    square_flat = summed[2]
    grad_norm = jnp.sqrt(jnp.sum(gradient * gradient))
    shrink = jnp.minimum(1.0, clip_norm / (grad_norm + 1e-06))
    grad_row = (
        jnp.where(
            valid,
            lax.dynamic_slice_in_dim(jnp.concatenate([gradient, padding]), row_begin, slot_cap),
            0.0,
        )
        * shrink
    )
    new_mean = beta_one * adam_mean[0] + (1.0 - beta_one) * grad_row
    new_square = beta_two * adam_square[0] + (1.0 - beta_two) * grad_row * grad_row
    grad_flat = gradient * shrink
    mean_all = beta_one * mean_flat + (1.0 - beta_one) * grad_flat
    square_all = beta_two * square_flat + (1.0 - beta_two) * grad_flat * grad_flat
    direction = (
        mean_all
        / (1.0 - beta_one**step_count)
        / (jnp.sqrt(square_all / (1.0 - beta_two**step_count)) + adam_eps)
    )
    new_params = parameters - learn_rate * direction
    return (
        normed,
        grad_hidden,
        grad_gating,
        grad_dt,
        grad_b,
        grad_c,
        new_params,
        new_mean[None],
        new_square[None],
    )


def solution(mesh):
    return jax.shard_map(
        on_device,
        mesh=mesh,
        in_specs=(
            P("dp", "ctx", None),
            P("dp", "ctx", None),
            P("dp", "ctx", None),
            P("dp", "ctx", None),
            P("dp", "ctx", None),
            P("dp", None),
            P("dp", "ctx", None),
            P(),
            P("dp", None),
            P("dp", None),
            P(),
            P(),
        ),
        out_specs=(
            P("dp", "ctx", None),
            P("dp", "ctx", None),
            P("dp", "ctx", None),
            P("dp", "ctx", None),
            P("dp", "ctx", None),
            P("dp", "ctx", None),
            P(),
            P("dp", None),
            P("dp", None),
        ),
        check_vma=False,
    )
```

```python
import jax
import jax.numpy as jnp
from jax import lax
from jax.sharding import PartitionSpec as P

SPAN = 256
CH = 3072


eps_norm = 1e-05
clip_norm = 64.0
beta_one = 0.9
beta_two = 0.95
adam_eps = 1e-08
learn_rate = 0.02
step_count = 100.0
highest = lax.Precision.HIGHEST


def to_heads(x, groups):
    _, t, c = x.shape
    x = x.reshape(t, groups, c // groups).transpose(1, 0, 2)
    x = lax.all_to_all(x, "ctx", 0, 0, tiled=True)
    return x.reshape(groups * t, c // groups)


def from_heads(x, groups):
    tw, w = x.shape
    x = x.reshape(groups, tw // groups, w)
    return lax.all_to_all(x, "ctx", 0, 0, tiled=True)


def to_positions(x, groups):
    parts = from_heads(x, groups)
    _, t, w = parts.shape
    return parts.transpose(1, 0, 2).reshape(1, t, groups * w)


def tree_sum(x, axis):
    size = lax.axis_size(axis)
    if size & (size - 1):
        return lax.psum(x, axis)
    step = 1
    while step < size:
        x = x + lax.ppermute(x, axis, [(i, i ^ step) for i in range(size)])
        step *= 2
    return x


def rounded(value):
    return lax.optimization_barrier(value.astype(jnp.bfloat16)).astype(jnp.float32)


def ssd_group(hidden, dt_raw, b_input, c_input, resets, a_log, dt_bias, skip):
    length = hidden.shape[0]
    heads = a_log.shape[0]
    width = hidden.shape[1] // heads
    blocks = length // SPAN
    step_sizes = jax.nn.softplus(dt_raw.astype(jnp.float32) + dt_bias)
    log_decay = (step_sizes * -jnp.exp(a_log)).reshape(blocks, SPAN, heads).transpose(0, 2, 1)
    lower = (jnp.arange(SPAN)[:, None] >= jnp.arange(SPAN)[None, :]).astype(jnp.float32)
    cumul = jnp.einsum("chs,ts->cht", log_decay, lower, precision=highest)
    inputs = hidden.astype(jnp.float32).reshape(blocks, SPAN, heads, width)
    scaled = rounded(inputs * step_sizes.reshape(blocks, SPAN, heads, 1))
    b_rows = b_input.astype(jnp.float32).reshape(blocks, SPAN, -1)
    c_rows = c_input.astype(jnp.float32).reshape(blocks, SPAN, -1)
    scores = jnp.einsum("ctn,csn->cts", c_rows, b_rows, precision=highest)
    causal = jnp.arange(SPAN)[:, None] >= jnp.arange(SPAN)[None, :]
    spread = cumul[:, :, :, None] - cumul[:, :, None, :]
    decay = jnp.where(causal, jnp.exp(jnp.where(causal, spread, 0.0)), 0.0)
    weights = rounded(scores[:, None] * decay)
    intra = jnp.einsum("chts,cshp->cthp", weights, scaled, precision=highest)
    tail = cumul[:, :, -1:] - cumul
    b_decayed = rounded(b_rows[:, None] * jnp.exp(tail)[..., None])
    block_state = jnp.einsum("chsn,cshp->chnp", b_decayed, scaled, precision=highest)
    keep = 1.0 - resets.astype(jnp.float32)

    def advance(state, items):
        keep_one, total, added = items
        entering = state * keep_one
        return (jnp.exp(total)[:, None, None] * entering + added, entering)

    start_state = jnp.zeros(block_state.shape[1:], jnp.float32)
    _, entering = lax.scan(advance, start_state, (keep, cumul[:, :, -1], block_state), unroll=True)
    c_decayed = rounded(c_rows[:, None] * jnp.exp(cumul)[..., None])
    inter = jnp.einsum("chtn,chnp->cthp", c_decayed, rounded(entering), precision=highest)
    output = intra + inter + skip[:, None] * inputs
    return output.reshape(length, heads * width).astype(jnp.bfloat16)


def gate_values(y_values, gating):
    gated = y_values.astype(jnp.float32) * jax.nn.silu(gating.astype(jnp.float32))
    return (gated, jnp.sum(gated * gated, axis=-1))


def normalize(gated, total, gain):
    factor = lax.rsqrt(total / CH + eps_norm)
    return (factor, (gated * factor[..., None] * gain).astype(jnp.bfloat16))


def norm_backward(cotangent, gain, gated, factor, dot_total, y_values, gating):
    upstream = cotangent.astype(jnp.float32) * gain
    d_gated = (
        upstream * factor[..., None]
        - gated * (factor * factor * factor * dot_total / CH)[..., None]
    )
    gate_f = gating.astype(jnp.float32)
    sigma = jax.nn.sigmoid(gate_f)
    d_y = (d_gated * (gate_f * sigma)).astype(jnp.bfloat16)
    d_gate = (
        d_gated * y_values.astype(jnp.float32) * sigma * (1.0 + gate_f * (1.0 - sigma))
    ).astype(jnp.bfloat16)
    d_gain = jnp.sum(
        cotangent.astype(jnp.float32) * gated * factor[..., None], axis=tuple(range(gated.ndim - 1))
    )
    return (d_y, d_gate, d_gain)


def on_device(
    hidden,
    gating,
    dt_raw,
    b_input,
    c_input,
    resets,
    cotangent,
    parameters,
    adam_mean,
    adam_square,
    bucket_size,
    bucket_owner,
):
    heads_all = dt_raw.shape[2]
    groups = lax.axis_size("ctx")
    group = heads_all // groups
    state_size = b_input.shape[2]
    tokens = hidden.shape[1]
    first = lax.axis_index("ctx") * group
    head_params = parameters[: 3 * heads_all].reshape(3, heads_all)
    gain = parameters[3 * heads_all :]
    local_params = lax.dynamic_slice_in_dim(head_params, first, group, 1)
    width = hidden.shape[2] // groups
    shared = jnp.concatenate([b_input[0], c_input[0]], axis=1)
    small = jnp.concatenate(
        [
            jnp.broadcast_to(shared[None], (groups,) + shared.shape),
            dt_raw[0].reshape(tokens, groups, group).transpose(1, 0, 2),
        ],
        axis=2,
    )
    small_in = lax.all_to_all(small, "ctx", 0, 0, tiled=True).reshape(groups * tokens, -1)
    x_in = to_heads(hidden, groups)
    b_all = small_in[None, :, :state_size]
    c_all = small_in[None, :, state_size : 2 * state_size]
    seq_resets = resets[0]

    def local_fn(x_arg, dt_arg, b_arg, c_arg, a_arg, bias_arg, skip_arg):
        return ssd_group(x_arg, dt_arg, b_arg, c_arg, seq_resets, a_arg, bias_arg, skip_arg)

    x_heads = x_in[None]
    dt_heads = small_in[None, :, 2 * state_size :]
    y_heads, pullback = jax.vjp(
        local_fn,
        x_heads[0],
        dt_heads[0],
        b_all[0],
        c_all[0],
        local_params[0],
        local_params[1],
        local_params[2],
    )
    y_seq = to_positions(y_heads, groups)
    gated, total = gate_values(y_seq, gating)
    factor, normed = normalize(gated, total, gain)
    dot_total = jnp.sum(cotangent.astype(jnp.float32) * gain * gated, axis=-1)
    d_y, grad_gating, d_gain = norm_backward(
        cotangent, gain, gated, factor, dot_total, y_seq, gating
    )
    d_y_heads = to_heads(d_y, groups)[None]
    d_x, d_dt, d_b, d_c, d_alog, d_bias, d_skip = pullback(d_y_heads[0])
    back = from_heads(jnp.concatenate([d_x, d_b, d_c, d_dt], axis=-1), groups)
    grad_hidden = back[..., :width].transpose(1, 0, 2).reshape(1, tokens, groups * width)
    grad_dt = back[..., width + 2 * state_size :].transpose(1, 0, 2).reshape(1, tokens, heads_all)
    pair_sum = jnp.sum(
        back[..., width : width + 2 * state_size].astype(jnp.float32), axis=0
    )[None].astype(jnp.bfloat16)
    grad_b = pair_sum[..., :state_size]
    grad_c = pair_sum[..., state_size:]
    head_grads = jnp.stack([d_alog, d_bias, d_skip])
    full_heads = lax.dynamic_update_slice(
        jnp.zeros((3, heads_all), jnp.float32), head_grads, (0, first)
    )
    grad_part = jnp.concatenate([full_heads.reshape(-1), d_gain])
    owners = lax.axis_size("dp")
    slot_cap = adam_mean.shape[1]
    total_len = parameters.shape[0]
    ends = jnp.cumsum(bucket_size)
    begins = ends - bucket_size
    order = jnp.arange(owners, dtype=jnp.int32)
    mine = lax.axis_index("dp")
    my_bucket = jnp.sum(jnp.where(bucket_owner == mine, order, 0))
    row_begin = jnp.sum(jnp.where(order == my_bucket, begins, 0))
    row_size = jnp.sum(jnp.where(order == my_bucket, bucket_size, 0))
    slots = jnp.arange(slot_cap, dtype=jnp.int32)
    valid = slots < row_size
    padding = jnp.zeros((slot_cap,), jnp.float32)
    own_state = jnp.where(valid, jnp.stack([adam_mean[0], adam_square[0]]), 0.0)
    laid = lax.dynamic_update_slice(
        jnp.zeros((2, total_len + slot_cap), jnp.float32), own_state, (0, row_begin)
    )[:, :total_len]
    summed = tree_sum(jnp.concatenate([grad_part[None], laid]), "dp")
    gradient = tree_sum(summed[0], "ctx")
    mean_flat = summed[1]
    square_flat = summed[2]
    grad_norm = jnp.sqrt(jnp.sum(gradient * gradient))
    shrink = jnp.minimum(1.0, clip_norm / (grad_norm + 1e-06))
    grad_row = (
        jnp.where(
            valid,
            lax.dynamic_slice_in_dim(jnp.concatenate([gradient, padding]), row_begin, slot_cap),
            0.0,
        )
        * shrink
    )
    new_mean = beta_one * adam_mean[0] + (1.0 - beta_one) * grad_row
    new_square = beta_two * adam_square[0] + (1.0 - beta_two) * grad_row * grad_row
    grad_flat = gradient * shrink
    mean_all = beta_one * mean_flat + (1.0 - beta_one) * grad_flat
    square_all = beta_two * square_flat + (1.0 - beta_two) * grad_flat * grad_flat
    direction = (
        mean_all
        / (1.0 - beta_one**step_count)
        / (jnp.sqrt(square_all / (1.0 - beta_two**step_count)) + adam_eps)
    )
    new_params = parameters - learn_rate * direction
    return (
        normed,
        grad_hidden,
        grad_gating,
        grad_dt,
        grad_b,
        grad_c,
        new_params,
        new_mean[None],
        new_square[None],
    )


def solution(mesh):
    return jax.shard_map(
        on_device,
        mesh=mesh,
        in_specs=(
            P("dp", "ctx", None),
            P("dp", "ctx", None),
            P("dp", "ctx", None),
            P("dp", "ctx", None),
            P("dp", "ctx", None),
            P("dp", None),
            P("dp", "ctx", None),
            P(),
            P("dp", None),
            P("dp", None),
            P(),
            P(),
        ),
        out_specs=(
            P("dp", "ctx", None),
            P("dp", "ctx", None),
            P("dp", "ctx", None),
            P("dp", "ctx", None),
            P("dp", "ctx", None),
            P("dp", "ctx", None),
            P(),
            P("dp", None),
            P("dp", None),
        ),
        check_vma=False,
    )
```
